128 devices in a mesh: row: 16 (over x, y), col: 8 (over z, core).
Axes of the slice: x: 4, y: 4, z: 4, core: 2. Of those that a mesh axis runs over, the one named last changes fastest.
Arguments:
- pattern_in: int32 [64, 16], replicated, may hold values from 0 to 63, as said below
- pattern_mid: int32 [64, 16], replicated, may hold values from 0 to 63, as said below
- pattern_out: int32 [64, 16], replicated, may hold values from 0 to 63, as said below
- density_blocks: float32 [4, 16, 2, 8, 256, 256], P(None, 'row', None, 'col'), as said below
Outputs:
- purified_blocks: float32 [4, 16, 2, 8, 256, 256], P(None, 'row', None, 'col')
The draws below stay inside these ranges and needn't reach their ends.
Inputs may be any that keep to these rules, and one draw needn't show every extreme that they name: `pattern_in`: slot l * 8 + c of block row I names a block column congruent to c modulo 8; no column stands twice in a row; slot I mod 8 of row I names I; J stands in row I exactly when I stands in row J. `pattern_mid`: as for pattern_in. `pattern_out`: as for pattern_in. `density_blocks`: the block of row J for column I is the transpose of the block of row I for column J.
All inputs are finite; a program needn't handle non-finite values.
Results may differ from the reference program's by a relative error of at most 0.0091.
Values may be sent and summed in bfloat16 or wider, within the bound.
No kernel may reach another device: no remote copies, remote signals or barrier semaphores. Data moves between devices by JAX's collectives and lax.ppermute only.
A program may use at most 128 MiB of HBM per device.

```python
import jax
import jax.numpy as jnp
from jax import lax

BS = 256
BR = 4
LZ = 2
ITERS = 2
GRID_ROWS = 16
GRID_COLS = 8
NB = 64
NZ = 16
OCC = 8192


def make_pattern(seed_key):
    classes = NZ // LZ
    members = NB // classes
    row_ids = jnp.arange(NB, dtype=jnp.int32)[:, None, None]
    slot_ids = jnp.arange(LZ, dtype=jnp.int32)[None, :, None]
    target_class = jnp.arange(classes, dtype=jnp.int32)[None, None, :]
    residue = row_ids % classes
    offset_in = row_ids // classes

    def one_perm(pair_id):
        return jax.random.permutation(jax.random.fold_in(seed_key, pair_id), members).astype(jnp.int32)
    perms = jax.vmap(one_perm)(jnp.arange(classes * classes, dtype=jnp.int32)).reshape(classes, classes, members)
    inverse = jnp.argsort(perms, axis=-1).astype(jnp.int32)
    forward = perms[residue, target_class, (offset_in + slot_ids) % members]
    backward = (inverse[target_class, residue, offset_in] - slot_ids) % members
    position = inverse[residue, residue, offset_in]
    partner = perms[residue, residue, position ^ 1]
    same_class = jnp.where(slot_ids == 0, offset_in, partner)
    target_off = jnp.where(residue < target_class, forward, jnp.where(residue > target_class, backward, same_class))
    column = target_class + classes * target_off
    return column.reshape(NB, NZ).astype(jnp.int32)


def draw_pattern_in(key, part):
    return make_pattern(jax.random.fold_in(key, 101))


def draw_pattern_mid(key, part):
    return make_pattern(jax.random.fold_in(key, 102))


def draw_pattern_out(key, part):
    return make_pattern(jax.random.fold_in(key, 103))


def draw_density_blocks(key, part):
    listed = make_pattern(jax.random.fold_in(key, 101))
    classes = NZ // LZ
    grid_rows = NB // BR
    value_key = jax.random.fold_in(key, 7)
    scales = jnp.exp(jax.random.uniform(jax.random.fold_in(value_key, 1), (NB, BS), jnp.float32, jnp.log(0.8), jnp.log(1.25)))
    entry_base = jnp.exp(jax.random.uniform(jax.random.fold_in(value_key, 2), (NB, BS), jnp.float32, jnp.log(0.7), jnp.log(1.4)))
    row_factor = jnp.exp(jax.random.uniform(jax.random.fold_in(value_key, 3), (NB,), jnp.float32, jnp.log(0.6), jnp.log(1.67)))
    target = jax.random.uniform(jax.random.fold_in(value_key, 4), (), jnp.float32, 0.9, 0.95)
    noise_level = 0.6
    ramp = 3.0 - 2.0 * (jnp.arange(NB) % grid_rows).astype(jnp.float32) / max(grid_rows - 1, 1)
    weights = entry_base * (ramp * row_factor)[:, None]
    diag_vals = weights * (target * (NB * BS * 0.5) / jnp.sum(weights))
    sigma = noise_level / jnp.sqrt(jnp.float32(NZ * BS))
    row_grid = jnp.broadcast_to(jnp.arange(NB, dtype=jnp.int32)[:, None], (NB, NZ)).reshape(-1)
    col_grid = listed.reshape(-1)
    identity = jnp.eye(BS, dtype=jnp.float32)

    def one_block(row_id, col_id):
        low_id = jnp.minimum(row_id, col_id)
        high_id = jnp.maximum(row_id, col_id)
        noise = jax.random.normal(jax.random.fold_in(value_key, 10 + low_id * NB + high_id), (BS, BS), jnp.float32)
        noise = jnp.where(row_id > col_id, noise.T, noise)
        noise = jnp.where(row_id == col_id, (noise + noise.T) * 0.7071067811865476, noise)
        mixed = scales[row_id][:, None] * (sigma * noise) * scales[col_id][None, :]
        return mixed + jnp.where(row_id == col_id, identity * diag_vals[row_id][None, :], 0.0)
    blocks = jax.vmap(one_block)(row_grid, col_grid)
    return blocks.reshape(BR, grid_rows, LZ, classes, BS, BS).astype(jnp.float32)


def setup_inputs(seed: int = 0) -> dict:
    key_of = jax.random.split(jax.random.key(seed), 5)
    return {
        "pattern_in": draw_pattern_in(jax.random.fold_in(key_of[4], 71), 0),
        "pattern_mid": draw_pattern_mid(jax.random.fold_in(key_of[4], 71), 0),
        "pattern_out": draw_pattern_out(jax.random.fold_in(key_of[4], 71), 0),
        "density_blocks": draw_density_blocks(jax.random.fold_in(key_of[4], 71), 0),
    }


def row_product(panels, cur_list, next_list, row_id):
    inner = cur_list[row_id]
    inner_safe = jnp.maximum(inner, 0)
    targets = next_list[row_id]
    candidates = cur_list[inner_safe]
    matches = (candidates[None, :, :] == targets[:, None, None]) & (inner >= 0)[None, :, None] & (targets >= 0)[:, None, None]
    partner = jnp.einsum("okm,kmuv->okuv", matches.astype(jnp.float32), panels[inner_safe], precision=lax.Precision.HIGHEST)
    return jnp.einsum("kuv,okvw->ouw", panels[row_id], partner, precision=lax.Precision.HIGHEST)


def purify(values, cur_list, next_list):
    row_ids = jnp.arange(NB, dtype=jnp.int32)
    on_cur = cur_list == row_ids[:, None]
    trace_now = jnp.sum(jnp.where(on_cur, jnp.trace(values, axis1=2, axis2=3), 0.0))
    rounded = values.astype(jnp.bfloat16)
    rounded = lax.optimization_barrier(rounded)
    panels = rounded.astype(jnp.float32)
    product = lax.map(lambda row_id: row_product(panels, cur_list, next_list, row_id), row_ids)
    keep = (cur_list[:, None, :] == next_list[:, :, None]) & (next_list >= 0)[:, :, None]
    previous = jnp.einsum("iom,imuv->iouv", keep.astype(jnp.float32), values, precision=lax.Precision.HIGHEST)
    return jnp.where(trace_now > OCC, product, 2.0 * previous - product)


def reference(pattern_in, pattern_mid, pattern_out, density_blocks):
    all_lists = (pattern_in, pattern_mid, pattern_out)
    values = density_blocks.reshape(NB, NZ, BS, BS)
    for iteration in range(ITERS):
        values = purify(values, all_lists[iteration], all_lists[iteration + 1])
    return values.reshape(BR, GRID_ROWS, LZ, GRID_COLS, BS, BS)
```

```python
import functools

import jax
import jax.numpy as jnp
from jax import lax
from jax.experimental import pallas as pl
from jax.experimental.pallas import tpu as pltpu
from jax.sharding import PartitionSpec as P

ITERS = 2


def product_kernel(n_ref, o_ref, a_ref, b_ref, prev_ref, misc_ref,
                   rows_hbm, cols_hbm, owned_ref, out_ref, abuf, bbuf, sem):
    n = n_ref[0]
    out_ref[...] = jnp.zeros_like(out_ref)

    def copies(t, slot):
        ca = pltpu.make_async_copy(rows_hbm.at[a_ref[t]], abuf.at[slot], sem.at[0, slot])
        cb = pltpu.make_async_copy(cols_hbm.at[b_ref[t]], bbuf.at[slot], sem.at[1, slot])
        return ca, cb

    @pl.when(n > 0)
    def _():
        ca, cb = copies(0, 0)
        ca.start()
        cb.start()

    def body(t, carry):
        slot = t % 2
        ca, cb = copies(t, slot)
        ca.wait()
        cb.wait()

        @pl.when(t + 1 < n)
        def _():
            na, nb = copies(t + 1, 1 - slot)
            na.start()
            nb.start()

        o = o_ref[t]
        out_ref[o] += jnp.dot(abuf[slot], bbuf[slot], preferred_element_type=jnp.float32)
        return carry

    lax.fori_loop(0, n, body, 0)

    take_product = misc_ref[0] > 0
    for o in range(out_ref.shape[0]):
        p = prev_ref[o]
        prev = jnp.where(p >= 0, owned_ref[jnp.maximum(p, 0)], 0.0)
        acc = out_ref[o]
        out_ref[o] = jnp.where(take_product, acc, 2.0 * prev - acc)


def run_product(n, o_t, a_t, b_t, prev_t, misc, rows, cols, owned):
    nout, edge, _ = owned.shape
    max_terms = o_t.shape[0]
    grid_spec = pltpu.PrefetchScalarGridSpec(
        num_scalar_prefetch=6,
        grid=(1,),
        in_specs=[
            pl.BlockSpec(memory_space=pl.ANY),
            pl.BlockSpec(memory_space=pl.ANY),
            pl.BlockSpec((nout, edge, edge), lambda g, *refs: (0, 0, 0)),
        ],
        out_specs=pl.BlockSpec((nout, edge, edge), lambda g, *refs: (0, 0, 0)),
        scratch_shapes=[
            pltpu.VMEM((2, edge, edge), rows.dtype),
            pltpu.VMEM((2, edge, edge), cols.dtype),
            pltpu.SemaphoreType.DMA((2, 2)),
        ],
    )
    flops = 2 * edge * edge * edge * max_terms // 4
    cost = pl.CostEstimate(
        flops=flops, transcendentals=0, bytes_accessed=(max_terms // 2) * edge * edge * 4 + 3 * nout * edge * edge * 4
    )
    return pl.pallas_call(
        product_kernel,
        grid_spec=grid_spec,
        out_shape=jax.ShapeDtypeStruct(owned.shape, jnp.float32),
        cost_estimate=cost,
    )(n, o_t, a_t, b_t, prev_t, misc, rows, cols, owned)


def col_gather(x, grid_cols):
    plus2 = [(j, (j + 2) % grid_cols) for j in range(grid_cols)]
    minus2 = [(j, (j - 2) % grid_cols) for j in range(grid_cols)]
    sib = [(j, j ^ 1) for j in range(grid_cols)]
    half = x.shape[0] // 2
    from_minus = lax.ppermute(x, "col", plus2)
    from_plus = lax.ppermute(x, "col", minus2)
    sib_own = lax.ppermute(x, "col", sib)
    far_a = lax.ppermute(from_minus[:half], "col", plus2)
    far_b = lax.ppermute(from_plus[half:], "col", minus2)
    far = jnp.concatenate([far_a, far_b], axis=0)
    sib_near = lax.ppermute(jnp.stack([from_minus, from_plus]), "col", sib)
    sib_far = lax.ppermute(far, "col", sib)
    pieces = jnp.stack([x, from_minus, from_plus, far, sib_own, sib_near[0], sib_near[1], sib_far])
    return pieces


def piece_classes(col_index, grid_cols):
    j = col_index
    s = j ^ 1
    offs = jnp.stack([j, j - 2, j + 2, j + 4, s, s - 2, s + 2, s + 4])
    return offs % grid_cols


def purify_section(owned, cur_list, next_list, trace_now, grid_rows, grid_cols, row_index, col_index):
    block_rows = owned.shape[0]
    slot_pairs = owned.shape[2]
    edge = owned.shape[4]
    total_rows = cur_list.shape[0]
    slot_count = cur_list.shape[1]
    occupied = total_rows * edge / 2.0
    owned4 = owned.reshape(block_rows, slot_pairs, edge, edge)
    panels = owned4.astype(jnp.bfloat16)

    cols = lax.all_gather(panels, "row", axis=0, tiled=False)
    cols = cols.reshape(total_rows * slot_pairs, edge, edge)
    pieces = col_gather(panels, grid_cols)
    rows = pieces.reshape(grid_cols * block_rows * slot_pairs, edge, edge)

    cls = piece_classes(col_index, grid_cols)
    piece_of = jnp.zeros((grid_cols,), jnp.int32).at[cls].set(jnp.arange(grid_cols, dtype=jnp.int32))

    my_ids = jnp.arange(block_rows, dtype=jnp.int32) * grid_rows + row_index
    my_cur = cur_list[my_ids]
    my_next = next_list[my_ids]
    out_cols = my_next.reshape(block_rows, slot_pairs, grid_cols)[:, :, col_index]
    k_ids = jnp.arange(slot_count, dtype=jnp.int32)
    k_class = k_ids % grid_cols
    k_pair = k_ids // grid_cols
    a_idx = (piece_of[k_class][None, :] * block_rows + jnp.arange(block_rows, dtype=jnp.int32)[:, None]) * slot_pairs \
        + k_pair[None, :]
    inner = my_cur
    cand = cur_list.reshape(total_rows, slot_pairs, grid_cols)[:, :, col_index][inner]
    match = cand[:, None, :, :] == out_cols[:, :, None, None]
    valid = jnp.any(match, axis=-1)
    lsel = jnp.argmax(match, axis=-1).astype(jnp.int32)
    b_idx = ((inner % grid_rows) * block_rows + inner // grid_rows)[:, None, :] * slot_pairs + lsel
    nout = block_rows * slot_pairs
    o_ids = jnp.broadcast_to(jnp.arange(nout, dtype=jnp.int32).reshape(block_rows, slot_pairs, 1), valid.shape)
    a_full = jnp.broadcast_to(a_idx[:, None, :], valid.shape)
    flat_valid = valid.reshape(-1)
    order = jnp.argsort(jnp.logical_not(flat_valid), stable=True)
    n_terms = jnp.sum(flat_valid.astype(jnp.int32)).reshape(1)
    o_t = o_ids.reshape(-1)[order]
    a_t = a_full.reshape(-1)[order]
    b_t = b_idx.reshape(-1)[order]

    my_res = my_cur.reshape(block_rows, slot_pairs, grid_cols)[:, :, col_index]
    keep = my_res[:, None, :] == out_cols[:, :, None]
    prev_l = jnp.argmax(keep, axis=-1).astype(jnp.int32)
    prev_t = jnp.where(
        jnp.any(keep, axis=-1), jnp.arange(block_rows, dtype=jnp.int32)[:, None] * slot_pairs + prev_l, -1
    ).reshape(-1)
    misc = (trace_now > occupied).astype(jnp.int32).reshape(1)

    updated = run_product(n_terms, o_t, a_t, b_t, prev_t, misc, rows, cols, owned4.reshape(nout, edge, edge))
    return updated.reshape(block_rows, 1, slot_pairs, 1, edge, edge)


def local_trace(owned, cur_list, grid_rows, grid_cols, row_index, col_index):
    block_rows = owned.shape[0]
    slot_pairs = owned.shape[2]
    slot_count = cur_list.shape[1]
    own_index = jnp.arange(block_rows, dtype=jnp.int32) * grid_rows + row_index
    my_rows = cur_list[own_index]
    my_residue = my_rows.reshape(block_rows, slot_pairs, grid_cols)[:, :, col_index]
    owned_slots = owned[:, 0, :, 0]
    return jnp.sum(jnp.where(my_residue == own_index[:, None], jnp.trace(owned_slots, axis1=2, axis2=3), 0.0))


def shards(pattern_in, pattern_mid, pattern_out, density_blocks):
    grid_rows = lax.axis_size("row")
    grid_cols = lax.axis_size("col")
    row_index = lax.axis_index("row")
    col_index = lax.axis_index("col")
    all_lists = (pattern_in, pattern_mid, pattern_out)
    current = density_blocks
    for iteration in range(ITERS):
        diag_term = local_trace(current, all_lists[iteration], grid_rows, grid_cols, row_index, col_index)
        trace_now = lax.psum(diag_term, ("row", "col"))
        current = purify_section(
            current, all_lists[iteration], all_lists[iteration + 1], trace_now,
            grid_rows, grid_cols, row_index, col_index,
        )
    return current


def solution(mesh):
    in_specs = (P(), P(), P(), P(None, "row", None, "col", None, None))
    out_specs = P(None, "row", None, "col", None, None)
    return jax.shard_map(shards, mesh=mesh, in_specs=in_specs, out_specs=out_specs, check_vma=False)
```

```python
import jax
import jax.numpy as jnp
from jax import lax
from jax.experimental import pallas as pl
from jax.experimental.pallas import tpu as pltpu
from jax.sharding import PartitionSpec as P

ITERS = 2


def product_kernel(n_ref, o_ref, a_ref, b_ref, prev_ref, misc_ref, rows_ref, cols_ref, owned_ref, out_ref):
    out_ref[...] = jnp.zeros_like(out_ref)

    def body(t, carry):
        o = o_ref[t]
        out_ref[o] += jnp.dot(rows_ref[a_ref[t]], cols_ref[b_ref[t]], preferred_element_type=jnp.float32)
        return carry

    lax.fori_loop(0, n_ref[0], body, 0)

    take_product = misc_ref[0] > 0
    for o in range(out_ref.shape[0]):
        p = prev_ref[o]
        prev = jnp.where(p >= 0, owned_ref[jnp.maximum(p, 0)], 0.0)
        acc = out_ref[o]
        out_ref[o] = jnp.where(take_product, acc, 2.0 * prev - acc)


def run_product(n, o_t, a_t, b_t, prev_t, misc, rows, cols, owned):
    nout, edge, _ = owned.shape
    max_terms = o_t.shape[0]
    smem = pl.BlockSpec(memory_space=pltpu.SMEM)
    vmem = pl.BlockSpec(memory_space=pltpu.VMEM)
    flops = 2 * edge * edge * edge * max_terms // 4
    nbytes = (rows.size + cols.size) * 2 + 2 * owned.size * 4
    return pl.pallas_call(
        product_kernel,
        in_specs=[smem] * 6 + [vmem] * 3,
        out_specs=vmem,
        out_shape=jax.ShapeDtypeStruct(owned.shape, jnp.float32),
        cost_estimate=pl.CostEstimate(flops=flops, transcendentals=0, bytes_accessed=nbytes),
        compiler_params=pltpu.CompilerParams(vmem_limit_bytes=48 * 1024 * 1024),
    )(n, o_t, a_t, b_t, prev_t, misc, rows, cols, owned)


def col_gather(x, grid_cols):
    plus2 = [(j, (j + 2) % grid_cols) for j in range(grid_cols)]
    minus2 = [(j, (j - 2) % grid_cols) for j in range(grid_cols)]
    sib = [(j, j ^ 1) for j in range(grid_cols)]
    half = x.shape[0] // 2
    from_minus = lax.ppermute(x, "col", plus2)
    from_plus = lax.ppermute(x, "col", minus2)
    sib_own = lax.ppermute(x, "col", sib)
    far_a = lax.ppermute(from_minus[:half], "col", plus2)
    far_b = lax.ppermute(from_plus[half:], "col", minus2)
    far = jnp.concatenate([far_a, far_b], axis=0)
    sib_near = lax.ppermute(jnp.stack([from_minus, from_plus]), "col", sib)
    sib_far = lax.ppermute(far, "col", sib)
    pieces = jnp.stack([x, from_minus, from_plus, far, sib_own, sib_near[0], sib_near[1], sib_far])
    return pieces


def piece_classes(col_index, grid_cols):
    j = col_index
    s = j ^ 1
    offs = jnp.stack([j, j - 2, j + 2, j + 4, s, s - 2, s + 2, s + 4])
    return offs % grid_cols


def purify_section(owned, cur_list, next_list, trace_now, grid_rows, grid_cols, row_index, col_index):
    block_rows = owned.shape[0]
    slot_pairs = owned.shape[2]
    edge = owned.shape[4]
    total_rows = cur_list.shape[0]
    slot_count = cur_list.shape[1]
    occupied = total_rows * edge / 2.0
    owned4 = owned.reshape(block_rows, slot_pairs, edge, edge)
    panels = owned4.astype(jnp.bfloat16)

    cols = lax.all_gather(panels, "row", axis=0, tiled=False)
    cols = cols.reshape(total_rows * slot_pairs, edge, edge)
    pieces = col_gather(panels, grid_cols)
    rows = pieces.reshape(grid_cols * block_rows * slot_pairs, edge, edge)

    cls = piece_classes(col_index, grid_cols)
    piece_of = jnp.zeros((grid_cols,), jnp.int32).at[cls].set(jnp.arange(grid_cols, dtype=jnp.int32))

    my_ids = jnp.arange(block_rows, dtype=jnp.int32) * grid_rows + row_index
    my_cur = cur_list[my_ids]
    my_next = next_list[my_ids]
    out_cols = my_next.reshape(block_rows, slot_pairs, grid_cols)[:, :, col_index]
    k_ids = jnp.arange(slot_count, dtype=jnp.int32)
    k_class = k_ids % grid_cols
    k_pair = k_ids // grid_cols
    a_idx = (piece_of[k_class][None, :] * block_rows + jnp.arange(block_rows, dtype=jnp.int32)[:, None]) * slot_pairs \
        + k_pair[None, :]
    inner = my_cur
    cand = cur_list.reshape(total_rows, slot_pairs, grid_cols)[:, :, col_index][inner]
    match = cand[:, None, :, :] == out_cols[:, :, None, None]
    valid = jnp.any(match, axis=-1)
    lsel = jnp.argmax(match, axis=-1).astype(jnp.int32)
    b_idx = ((inner % grid_rows) * block_rows + inner // grid_rows)[:, None, :] * slot_pairs + lsel
    nout = block_rows * slot_pairs
    o_ids = jnp.broadcast_to(jnp.arange(nout, dtype=jnp.int32).reshape(block_rows, slot_pairs, 1), valid.shape)
    a_full = jnp.broadcast_to(a_idx[:, None, :], valid.shape)
    flat_valid = valid.reshape(-1)
    order = jnp.argsort(jnp.logical_not(flat_valid), stable=True)
    n_terms = jnp.sum(flat_valid.astype(jnp.int32)).reshape(1)
    o_t = o_ids.reshape(-1)[order]
    a_t = a_full.reshape(-1)[order]
    b_t = b_idx.reshape(-1)[order]

    my_res = my_cur.reshape(block_rows, slot_pairs, grid_cols)[:, :, col_index]
    keep = my_res[:, None, :] == out_cols[:, :, None]
    prev_l = jnp.argmax(keep, axis=-1).astype(jnp.int32)
    prev_t = jnp.where(
        jnp.any(keep, axis=-1), jnp.arange(block_rows, dtype=jnp.int32)[:, None] * slot_pairs + prev_l, -1
    ).reshape(-1)
    misc = (trace_now > occupied).astype(jnp.int32).reshape(1)

    updated = run_product(n_terms, o_t, a_t, b_t, prev_t, misc, rows, cols, owned4.reshape(nout, edge, edge))
    return updated.reshape(block_rows, 1, slot_pairs, 1, edge, edge)


def local_trace(owned, cur_list, grid_rows, grid_cols, row_index, col_index):
    block_rows = owned.shape[0]
    slot_pairs = owned.shape[2]
    slot_count = cur_list.shape[1]
    own_index = jnp.arange(block_rows, dtype=jnp.int32) * grid_rows + row_index
    my_rows = cur_list[own_index]
    my_residue = my_rows.reshape(block_rows, slot_pairs, grid_cols)[:, :, col_index]
    owned_slots = owned[:, 0, :, 0]
    return jnp.sum(jnp.where(my_residue == own_index[:, None], jnp.trace(owned_slots, axis1=2, axis2=3), 0.0))


def shards(pattern_in, pattern_mid, pattern_out, density_blocks):
    grid_rows = lax.axis_size("row")
    grid_cols = lax.axis_size("col")
    row_index = lax.axis_index("row")
    col_index = lax.axis_index("col")
    all_lists = (pattern_in, pattern_mid, pattern_out)
    current = density_blocks
    for iteration in range(ITERS):
        diag_term = local_trace(current, all_lists[iteration], grid_rows, grid_cols, row_index, col_index)
        trace_now = lax.psum(lax.psum(diag_term, "col"), "row")
        current = purify_section(
            current, all_lists[iteration], all_lists[iteration + 1], trace_now,
            grid_rows, grid_cols, row_index, col_index,
        )
    return current


def solution(mesh):
    in_specs = (P(), P(), P(), P(None, "row", None, "col", None, None))
    out_specs = P(None, "row", None, "col", None, None)
    return jax.shard_map(shards, mesh=mesh, in_specs=in_specs, out_specs=out_specs, check_vma=False)
```

```python
import jax
import jax.numpy as jnp
from jax import lax
from jax.experimental import pallas as pl
from jax.experimental.pallas import tpu as pltpu
from jax.sharding import PartitionSpec as P

ITERS = 2


def product_kernel(a_ref, b_ref, v_ref, prev_ref, misc_ref, rows_ref, cols_ref, owned_ref, out_ref):
    nout = out_ref.shape[0]
    terms = a_ref.shape[0] // nout
    take_product = misc_ref[0] > 0

    def body(o, carry):
        acc = None
        for k in range(terms):
            t = o * terms + k
            d = jnp.dot(rows_ref[a_ref[t]], cols_ref[b_ref[t]], preferred_element_type=jnp.float32)
            d = jnp.where(v_ref[t] > 0, d, 0.0)
            acc = d if acc is None else acc + d
        p = prev_ref[o]
        prev = jnp.where(p >= 0, owned_ref[jnp.maximum(p, 0)], 0.0)
        out_ref[o] = jnp.where(take_product, acc, 2.0 * prev - acc)
        return carry

    lax.fori_loop(0, nout, body, 0)


def run_product(a_t, b_t, v_t, prev_t, misc, rows, cols, owned):
    nout, edge, _ = owned.shape
    max_terms = a_t.shape[0]
    smem = pl.BlockSpec(memory_space=pltpu.SMEM)
    vmem = pl.BlockSpec(memory_space=pltpu.VMEM)
    flops = 2 * edge * edge * edge * max_terms
    nbytes = (rows.size + cols.size) * 2 + 2 * owned.size * 4
    return pl.pallas_call(
        product_kernel,
        in_specs=[smem] * 5 + [vmem] * 3,
        out_specs=vmem,
        out_shape=jax.ShapeDtypeStruct(owned.shape, jnp.float32),
        cost_estimate=pl.CostEstimate(flops=flops, transcendentals=0, bytes_accessed=nbytes),
        compiler_params=pltpu.CompilerParams(vmem_limit_bytes=48 * 1024 * 1024),
    )(a_t, b_t, v_t, prev_t, misc, rows, cols, owned)


def col_gather(x, grid_cols):
    plus2 = [(j, (j + 2) % grid_cols) for j in range(grid_cols)]
    minus2 = [(j, (j - 2) % grid_cols) for j in range(grid_cols)]
    sib = [(j, j ^ 1) for j in range(grid_cols)]
    half = x.shape[0] // 2
    from_minus = lax.ppermute(x, "col", plus2)
    from_plus = lax.ppermute(x, "col", minus2)
    sib_own = lax.ppermute(x, "col", sib)
    far_a = lax.ppermute(from_minus[:half], "col", plus2)
    far_b = lax.ppermute(from_plus[half:], "col", minus2)
    far = jnp.concatenate([far_a, far_b], axis=0)
    sib_near = lax.ppermute(jnp.stack([from_minus, from_plus]), "col", sib)
    sib_far = lax.ppermute(far, "col", sib)
    pieces = jnp.stack([x, from_minus, from_plus, far, sib_own, sib_near[0], sib_near[1], sib_far])
    return pieces


def piece_classes(col_index, grid_cols):
    j = col_index
    s = j ^ 1
    offs = jnp.stack([j, j - 2, j + 2, j + 4, s, s - 2, s + 2, s + 4])
    return offs % grid_cols


def purify_section(owned, cur_list, next_list, trace_now, grid_rows, grid_cols, row_index, col_index):
    block_rows = owned.shape[0]
    slot_pairs = owned.shape[2]
    edge = owned.shape[4]
    total_rows = cur_list.shape[0]
    slot_count = cur_list.shape[1]
    occupied = total_rows * edge / 2.0
    owned4 = owned.reshape(block_rows, slot_pairs, edge, edge)
    panels = owned4.astype(jnp.bfloat16)

    cols = lax.all_gather(panels, "row", axis=0, tiled=False)
    cols = cols.reshape(total_rows * slot_pairs, edge, edge)
    pieces = col_gather(panels, grid_cols)
    rows = pieces.reshape(grid_cols * block_rows * slot_pairs, edge, edge)

    cls = piece_classes(col_index, grid_cols)
    piece_of = jnp.zeros((grid_cols,), jnp.int32).at[cls].set(jnp.arange(grid_cols, dtype=jnp.int32))

    my_ids = jnp.arange(block_rows, dtype=jnp.int32) * grid_rows + row_index
    my_cur = cur_list[my_ids]
    my_next = next_list[my_ids]
    out_cols = my_next.reshape(block_rows, slot_pairs, grid_cols)[:, :, col_index]
    k_ids = jnp.arange(slot_count, dtype=jnp.int32)
    k_class = k_ids % grid_cols
    k_pair = k_ids // grid_cols
    a_idx = (piece_of[k_class][None, :] * block_rows + jnp.arange(block_rows, dtype=jnp.int32)[:, None]) * slot_pairs \
        + k_pair[None, :]
    inner = my_cur
    cand = cur_list.reshape(total_rows, slot_pairs, grid_cols)[:, :, col_index][inner]
    match = cand[:, None, :, :] == out_cols[:, :, None, None]
    valid = jnp.any(match, axis=-1)
    lsel = jnp.argmax(match, axis=-1).astype(jnp.int32)
    b_idx = ((inner % grid_rows) * block_rows + inner // grid_rows)[:, None, :] * slot_pairs + lsel
    nout = block_rows * slot_pairs
    a_t = jnp.broadcast_to(a_idx[:, None, :], valid.shape).reshape(-1)
    b_t = b_idx.reshape(-1)
    v_t = valid.astype(jnp.int32).reshape(-1)

    my_res = my_cur.reshape(block_rows, slot_pairs, grid_cols)[:, :, col_index]
    keep = my_res[:, None, :] == out_cols[:, :, None]
    prev_l = jnp.argmax(keep, axis=-1).astype(jnp.int32)
    prev_t = jnp.where(
        jnp.any(keep, axis=-1), jnp.arange(block_rows, dtype=jnp.int32)[:, None] * slot_pairs + prev_l, -1
    ).reshape(-1)
    misc = (trace_now > occupied).astype(jnp.int32).reshape(1)

    updated = run_product(a_t, b_t, v_t, prev_t, misc, rows, cols, owned4.reshape(nout, edge, edge))
    return updated.reshape(block_rows, 1, slot_pairs, 1, edge, edge)


def local_trace(owned, cur_list, grid_rows, grid_cols, row_index, col_index):
    block_rows = owned.shape[0]
    slot_pairs = owned.shape[2]
    slot_count = cur_list.shape[1]
    own_index = jnp.arange(block_rows, dtype=jnp.int32) * grid_rows + row_index
    my_rows = cur_list[own_index]
    my_residue = my_rows.reshape(block_rows, slot_pairs, grid_cols)[:, :, col_index]
    owned_slots = owned[:, 0, :, 0]
    return jnp.sum(jnp.where(my_residue == own_index[:, None], jnp.trace(owned_slots, axis1=2, axis2=3), 0.0))


def shards(pattern_in, pattern_mid, pattern_out, density_blocks):
    grid_rows = lax.axis_size("row")
    grid_cols = lax.axis_size("col")
    row_index = lax.axis_index("row")
    col_index = lax.axis_index("col")
    all_lists = (pattern_in, pattern_mid, pattern_out)
    current = density_blocks
    for iteration in range(ITERS):
        diag_term = local_trace(current, all_lists[iteration], grid_rows, grid_cols, row_index, col_index)
        trace_now = lax.psum(lax.psum(diag_term, "col"), "row")
        current = purify_section(
            current, all_lists[iteration], all_lists[iteration + 1], trace_now,
            grid_rows, grid_cols, row_index, col_index,
        )
    return current


def solution(mesh):
    in_specs = (P(), P(), P(), P(None, "row", None, "col", None, None))
    out_specs = P(None, "row", None, "col", None, None)
    return jax.shard_map(shards, mesh=mesh, in_specs=in_specs, out_specs=out_specs, check_vma=False)
```

```python
import jax
import jax.numpy as jnp
from jax import lax
from jax.experimental import pallas as pl
from jax.experimental.pallas import tpu as pltpu
from jax.sharding import PartitionSpec as P

ITERS = 2


def product_kernel(a_ref, b_ref, v_ref, prev_ref, misc_ref, rows_hbm, cols_hbm, owned_ref,
                   out_ref, outb_ref, abuf, bbuf, asem, bsem):
    nout = out_ref.shape[0]
    terms = abuf.shape[1]
    per_row = 2
    nrows = nout // per_row
    take_product = misc_ref[0] > 0

    def a_copy(i, slot, k):
        return pltpu.make_async_copy(rows_hbm.at[a_ref[i * per_row * terms + k]], abuf.at[slot, k], asem.at[slot, k])

    def b_copy(o, slot, k):
        return pltpu.make_async_copy(cols_hbm.at[b_ref[o * terms + k]], bbuf.at[slot, k], bsem.at[slot, k])

    for k in range(terms):
        a_copy(0, 0, k).start()
        b_copy(0, 0, k).start()

    def body(o, carry):
        i = o // per_row
        first = o % per_row == 0
        aslot = i % 2
        bslot = o % 2

        @pl.when(first)
        def _():
            for k in range(terms):
                a_copy(i, aslot, k).wait()

            @pl.when(i + 1 < nrows)
            def _():
                for k in range(terms):
                    a_copy(i + 1, 1 - aslot, k).start()

        for k in range(terms):
            b_copy(o, bslot, k).wait()

        @pl.when(o + 1 < nout)
        def _():
            for k in range(terms):
                b_copy(o + 1, 1 - bslot, k).start()

        acc = None
        for k in range(terms):
            d = jnp.dot(abuf[aslot, k], bbuf[bslot, k], preferred_element_type=jnp.float32)
            d = jnp.where(v_ref[o * terms + k] > 0, d, 0.0)
            acc = d if acc is None else acc + d
        p = prev_ref[o]
        prev = jnp.where(p >= 0, owned_ref[jnp.maximum(p, 0)], 0.0)
        res = jnp.where(take_product, acc, 2.0 * prev - acc)
        out_ref[o] = res
        outb_ref[o] = res.astype(outb_ref.dtype)
        return carry

    lax.fori_loop(0, nout, body, 0)


def run_product(a_t, b_t, v_t, prev_t, misc, rows, cols, owned):
    nout, edge, _ = owned.shape
    max_terms = a_t.shape[0]
    terms = max_terms // nout
    smem = pl.BlockSpec(memory_space=pltpu.SMEM)
    vmem = pl.BlockSpec(memory_space=pltpu.VMEM)
    hbm = pl.BlockSpec(memory_space=pl.ANY)
    flops = 2 * edge * edge * edge * max_terms
    nbytes = (max_terms + max_terms // 2) * edge * edge * 2 + 2 * owned.size * 4
    return pl.pallas_call(
        product_kernel,
        in_specs=[smem] * 5 + [hbm, hbm, vmem],
        out_specs=(vmem, vmem),
        out_shape=(
            jax.ShapeDtypeStruct(owned.shape, jnp.float32),
            jax.ShapeDtypeStruct(owned.shape, jnp.bfloat16),
        ),
        scratch_shapes=[
            pltpu.VMEM((2, terms, edge, edge), rows.dtype),
            pltpu.VMEM((2, terms, edge, edge), cols.dtype),
            pltpu.SemaphoreType.DMA((2, terms)),
            pltpu.SemaphoreType.DMA((2, terms)),
        ],
        cost_estimate=pl.CostEstimate(flops=flops, transcendentals=0, bytes_accessed=nbytes),
        compiler_params=pltpu.CompilerParams(vmem_limit_bytes=48 * 1024 * 1024),
    )(a_t, b_t, v_t, prev_t, misc, rows, cols, owned)


def col_gather(x, grid_cols):
    plus2 = [(j, (j + 2) % grid_cols) for j in range(grid_cols)]
    minus2 = [(j, (j - 2) % grid_cols) for j in range(grid_cols)]
    sib = [(j, j ^ 1) for j in range(grid_cols)]
    half = x.shape[0] // 2
    from_minus = lax.ppermute(x, "col", plus2)
    from_plus = lax.ppermute(x, "col", minus2)
    sib_own = lax.ppermute(x, "col", sib)
    far_a = lax.ppermute(from_minus[:half], "col", plus2)
    far_b = lax.ppermute(from_plus[half:], "col", minus2)
    far = jnp.concatenate([far_a, far_b], axis=0)
    sib_near = lax.ppermute(jnp.stack([from_minus, from_plus]), "col", sib)
    sib_far = lax.ppermute(far, "col", sib)
    pieces = jnp.stack([x, from_minus, from_plus, far, sib_own, sib_near[0], sib_near[1], sib_far])
    return pieces


def piece_classes(col_index, grid_cols):
    j = col_index
    s = j ^ 1
    offs = jnp.stack([j, j - 2, j + 2, j + 4, s, s - 2, s + 2, s + 4])
    return offs % grid_cols


def purify_section(owned, panels, cur_list, next_list, trace_now, grid_rows, grid_cols, row_index, col_index):
    block_rows = owned.shape[0]
    slot_pairs = owned.shape[2]
    edge = owned.shape[4]
    total_rows = cur_list.shape[0]
    slot_count = cur_list.shape[1]
    occupied = total_rows * edge / 2.0
    owned4 = owned.reshape(block_rows, slot_pairs, edge, edge)
    panels = panels.reshape(block_rows, slot_pairs, edge, edge)

    cols = lax.all_gather(panels, "row", axis=0, tiled=False)
    cols = cols.reshape(total_rows * slot_pairs, edge, edge)
    pieces = col_gather(panels, grid_cols)
    rows = pieces.reshape(grid_cols * block_rows * slot_pairs, edge, edge)

    cls = piece_classes(col_index, grid_cols)
    piece_of = jnp.zeros((grid_cols,), jnp.int32).at[cls].set(jnp.arange(grid_cols, dtype=jnp.int32))

    my_ids = jnp.arange(block_rows, dtype=jnp.int32) * grid_rows + row_index
    my_cur = cur_list[my_ids]
    my_next = next_list[my_ids]
    out_cols = my_next.reshape(block_rows, slot_pairs, grid_cols)[:, :, col_index]
    k_ids = jnp.arange(slot_count, dtype=jnp.int32)
    k_class = k_ids % grid_cols
    k_pair = k_ids // grid_cols
    a_idx = (piece_of[k_class][None, :] * block_rows + jnp.arange(block_rows, dtype=jnp.int32)[:, None]) * slot_pairs \
        + k_pair[None, :]
    inner = my_cur
    cand = cur_list.reshape(total_rows, slot_pairs, grid_cols)[:, :, col_index][inner]
    match = cand[:, None, :, :] == out_cols[:, :, None, None]
    valid = jnp.any(match, axis=-1)
    lsel = jnp.argmax(match, axis=-1).astype(jnp.int32)
    b_idx = ((inner % grid_rows) * block_rows + inner // grid_rows)[:, None, :] * slot_pairs + lsel
    nout = block_rows * slot_pairs
    a_t = jnp.broadcast_to(a_idx[:, None, :], valid.shape).reshape(-1)
    b_t = b_idx.reshape(-1)
    v_t = valid.astype(jnp.int32).reshape(-1)

    my_res = my_cur.reshape(block_rows, slot_pairs, grid_cols)[:, :, col_index]
    keep = my_res[:, None, :] == out_cols[:, :, None]
    prev_l = jnp.argmax(keep, axis=-1).astype(jnp.int32)
    prev_t = jnp.where(
        jnp.any(keep, axis=-1), jnp.arange(block_rows, dtype=jnp.int32)[:, None] * slot_pairs + prev_l, -1
    ).reshape(-1)
    misc = (trace_now > occupied).astype(jnp.int32).reshape(1)

    updated, rounded = run_product(a_t, b_t, v_t, prev_t, misc, rows, cols, owned4.reshape(nout, edge, edge))
    return updated.reshape(owned.shape), rounded.reshape(owned.shape)


def local_trace(owned, cur_list, grid_rows, grid_cols, row_index, col_index):
    block_rows = owned.shape[0]
    slot_pairs = owned.shape[2]
    slot_count = cur_list.shape[1]
    own_index = jnp.arange(block_rows, dtype=jnp.int32) * grid_rows + row_index
    my_rows = cur_list[own_index]
    my_residue = my_rows.reshape(block_rows, slot_pairs, grid_cols)[:, :, col_index]
    owned_slots = owned[:, 0, :, 0]
    return jnp.sum(jnp.where(my_residue == own_index[:, None], jnp.trace(owned_slots, axis1=2, axis2=3), 0.0))


def shards(pattern_in, pattern_mid, pattern_out, density_blocks):
    grid_rows = lax.axis_size("row")
    grid_cols = lax.axis_size("col")
    row_index = lax.axis_index("row")
    col_index = lax.axis_index("col")
    all_lists = (pattern_in, pattern_mid, pattern_out)
    current = density_blocks
    rounded = density_blocks.astype(jnp.bfloat16)
    for iteration in range(ITERS):
        diag_term = local_trace(current, all_lists[iteration], grid_rows, grid_cols, row_index, col_index)
        trace_now = lax.psum(lax.psum(diag_term, "col"), "row")
        current, rounded = purify_section(
            current, rounded, all_lists[iteration], all_lists[iteration + 1], trace_now,
            grid_rows, grid_cols, row_index, col_index,
        )
    return current


def solution(mesh):
    in_specs = (P(), P(), P(), P(None, "row", None, "col", None, None))
    out_specs = P(None, "row", None, "col", None, None)
    return jax.shard_map(shards, mesh=mesh, in_specs=in_specs, out_specs=out_specs, check_vma=False)
```

```python
import jax
import jax.numpy as jnp
from jax import lax
from jax.experimental import pallas as pl
from jax.experimental.pallas import tpu as pltpu
from jax.sharding import PartitionSpec as P

ITERS = 2


def product_kernel(a_ref, b_ref, v_ref, prev_ref, misc_ref, rows_ref, cols_ref, owned_ref, out_ref, outb_ref):
    nout = out_ref.shape[0]
    terms = a_ref.shape[0] // nout
    take_product = misc_ref[0] > 0

    def body(o, carry):
        acc = None
        for k in range(terms):
            t = o * terms + k
            d = jnp.dot(rows_ref[a_ref[t]], cols_ref[b_ref[t]], preferred_element_type=jnp.float32)
            d = jnp.where(v_ref[t] > 0, d, 0.0)
            acc = d if acc is None else acc + d
        p = prev_ref[o]
        prev = jnp.where(p >= 0, owned_ref[jnp.maximum(p, 0)], 0.0)
        res = jnp.where(take_product, acc, 2.0 * prev - acc)
        out_ref[o] = res
        outb_ref[o] = res.astype(outb_ref.dtype)
        return carry

    lax.fori_loop(0, nout, body, 0)


def run_product(a_t, b_t, v_t, prev_t, misc, rows, cols, owned):
    nout, edge, _ = owned.shape
    max_terms = a_t.shape[0]
    smem = pl.BlockSpec(memory_space=pltpu.SMEM)
    vmem = pl.BlockSpec(memory_space=pltpu.VMEM)
    flops = 2 * edge * edge * edge * max_terms
    nbytes = (rows.size + cols.size) * 2 + 2 * owned.size * 4
    return pl.pallas_call(
        product_kernel,
        in_specs=[smem] * 5 + [vmem] * 3,
        out_specs=(vmem, vmem),
        out_shape=(
            jax.ShapeDtypeStruct(owned.shape, jnp.float32),
            jax.ShapeDtypeStruct(owned.shape, jnp.bfloat16),
        ),
        cost_estimate=pl.CostEstimate(flops=flops, transcendentals=0, bytes_accessed=nbytes),
        compiler_params=pltpu.CompilerParams(vmem_limit_bytes=48 * 1024 * 1024),
    )(a_t, b_t, v_t, prev_t, misc, rows, cols, owned)


def col_gather(x, grid_cols):
    plus2 = [(j, (j + 2) % grid_cols) for j in range(grid_cols)]
    minus2 = [(j, (j - 2) % grid_cols) for j in range(grid_cols)]
    sib = [(j, j ^ 1) for j in range(grid_cols)]
    half = x.shape[0] // 2
    from_minus = lax.ppermute(x, "col", plus2)
    from_plus = lax.ppermute(x, "col", minus2)
    sib_own = lax.ppermute(x, "col", sib)
    far_a = lax.ppermute(from_minus[:half], "col", plus2)
    far_b = lax.ppermute(from_plus[half:], "col", minus2)
    far = jnp.concatenate([far_a, far_b], axis=0)
    sib_near = lax.ppermute(jnp.stack([from_minus, from_plus]), "col", sib)
    sib_far = lax.ppermute(far, "col", sib)
    pieces = jnp.stack([x, from_minus, from_plus, far, sib_own, sib_near[0], sib_near[1], sib_far])
    return pieces


def piece_classes(col_index, grid_cols):
    j = col_index
    s = j ^ 1
    offs = jnp.stack([j, j - 2, j + 2, j + 4, s, s - 2, s + 2, s + 4])
    return offs % grid_cols


def purify_section(owned, panels, cur_list, next_list, trace_now, grid_rows, grid_cols, row_index, col_index):
    block_rows = owned.shape[0]
    slot_pairs = owned.shape[2]
    edge = owned.shape[4]
    total_rows = cur_list.shape[0]
    slot_count = cur_list.shape[1]
    occupied = total_rows * edge / 2.0
    owned4 = owned.reshape(block_rows, slot_pairs, edge, edge)
    panels = panels.reshape(block_rows, slot_pairs, edge, edge)

    cols = lax.all_gather(panels, "row", axis=0, tiled=False)
    cols = cols.reshape(total_rows * slot_pairs, edge, edge)
    pieces = col_gather(panels, grid_cols)
    rows = pieces.reshape(grid_cols * block_rows * slot_pairs, edge, edge)

    cls = piece_classes(col_index, grid_cols)
    piece_of = jnp.zeros((grid_cols,), jnp.int32).at[cls].set(jnp.arange(grid_cols, dtype=jnp.int32))

    my_ids = jnp.arange(block_rows, dtype=jnp.int32) * grid_rows + row_index
    my_cur = cur_list[my_ids]
    my_next = next_list[my_ids]
    out_cols = my_next.reshape(block_rows, slot_pairs, grid_cols)[:, :, col_index]
    k_ids = jnp.arange(slot_count, dtype=jnp.int32)
    k_class = k_ids % grid_cols
    k_pair = k_ids // grid_cols
    a_idx = (piece_of[k_class][None, :] * block_rows + jnp.arange(block_rows, dtype=jnp.int32)[:, None]) * slot_pairs \
        + k_pair[None, :]
    inner = my_cur
    cand = cur_list.reshape(total_rows, slot_pairs, grid_cols)[:, :, col_index][inner]
    match = cand[:, None, :, :] == out_cols[:, :, None, None]
    valid = jnp.any(match, axis=-1)
    lsel = jnp.argmax(match, axis=-1).astype(jnp.int32)
    b_idx = ((inner % grid_rows) * block_rows + inner // grid_rows)[:, None, :] * slot_pairs + lsel
    nout = block_rows * slot_pairs
    a_t = jnp.broadcast_to(a_idx[:, None, :], valid.shape).reshape(-1)
    b_t = b_idx.reshape(-1)
    v_t = valid.astype(jnp.int32).reshape(-1)

    my_res = my_cur.reshape(block_rows, slot_pairs, grid_cols)[:, :, col_index]
    keep = my_res[:, None, :] == out_cols[:, :, None]
    prev_l = jnp.argmax(keep, axis=-1).astype(jnp.int32)
    prev_t = jnp.where(
        jnp.any(keep, axis=-1), jnp.arange(block_rows, dtype=jnp.int32)[:, None] * slot_pairs + prev_l, -1
    ).reshape(-1)
    misc = (trace_now > occupied).astype(jnp.int32).reshape(1)

    updated, rounded = run_product(a_t, b_t, v_t, prev_t, misc, rows, cols, owned4.reshape(nout, edge, edge))
    return updated.reshape(owned.shape), rounded.reshape(owned.shape)


def local_trace(owned, cur_list, grid_rows, grid_cols, row_index, col_index):
    block_rows = owned.shape[0]
    slot_pairs = owned.shape[2]
    slot_count = cur_list.shape[1]
    own_index = jnp.arange(block_rows, dtype=jnp.int32) * grid_rows + row_index
    my_rows = cur_list[own_index]
    my_residue = my_rows.reshape(block_rows, slot_pairs, grid_cols)[:, :, col_index]
    owned_slots = owned[:, 0, :, 0]
    return jnp.sum(jnp.where(my_residue == own_index[:, None], jnp.trace(owned_slots, axis1=2, axis2=3), 0.0))


def shards(pattern_in, pattern_mid, pattern_out, density_blocks):
    grid_rows = lax.axis_size("row")
    grid_cols = lax.axis_size("col")
    row_index = lax.axis_index("row")
    col_index = lax.axis_index("col")
    all_lists = (pattern_in, pattern_mid, pattern_out)
    current = density_blocks
    rounded = density_blocks.astype(jnp.bfloat16)
    occupied = pattern_in.shape[0] * density_blocks.shape[-1] / 2.0
    diag_term = local_trace(current, pattern_in, grid_rows, grid_cols, row_index, col_index)
    wide = rounded.astype(jnp.float32)
    square_term = jnp.sum(wide * wide)
    totals = lax.psum(lax.psum(jnp.stack([diag_term, square_term]), "col"), "row")
    first_trace = totals[0]
    second_trace = jnp.where(first_trace > occupied, totals[1], 2.0 * first_trace - totals[1])
    traces = (first_trace, second_trace)
    for iteration in range(ITERS):
        current, rounded = purify_section(
            current, rounded, all_lists[iteration], all_lists[iteration + 1], traces[iteration],
            grid_rows, grid_cols, row_index, col_index,
        )
    return current


def solution(mesh):
    in_specs = (P(), P(), P(), P(None, "row", None, "col", None, None))
    out_specs = P(None, "row", None, "col", None, None)
    return jax.shard_map(shards, mesh=mesh, in_specs=in_specs, out_specs=out_specs, check_vma=False)
```

```python
import jax
import jax.numpy as jnp
from jax import lax
from jax.experimental import pallas as pl
from jax.experimental.pallas import tpu as pltpu
from jax.sharding import PartitionSpec as P

ITERS = 2


def product_kernel(a_ref, b_ref, v_ref, prev_ref, misc_ref, rows_ref, cols_ref, owned_ref, out_ref, outb_ref):
    nout = out_ref.shape[0]
    terms = a_ref.shape[0] // nout
    take_product = misc_ref[0] > 0

    def body(o, carry):
        acc = None
        for k in range(terms):
            t = o * terms + k
            d = jnp.dot(rows_ref[a_ref[t]], cols_ref[b_ref[t]], preferred_element_type=jnp.float32)
            acc = d if acc is None else acc + d
        p = prev_ref[o]
        prev = jnp.where(p >= 0, owned_ref[jnp.maximum(p, 0)], 0.0)
        res = jnp.where(take_product, acc, 2.0 * prev - acc)
        out_ref[o] = res
        outb_ref[o] = res.astype(outb_ref.dtype)
        return carry

    lax.fori_loop(0, nout, body, 0)


def run_product(a_t, b_t, v_t, prev_t, misc, rows, cols, owned):
    nout, edge, _ = owned.shape
    max_terms = a_t.shape[0]
    smem = pl.BlockSpec(memory_space=pltpu.SMEM)
    vmem = pl.BlockSpec(memory_space=pltpu.VMEM)
    flops = 2 * edge * edge * edge * max_terms
    nbytes = (rows.size + cols.size) * 2 + 2 * owned.size * 4
    return pl.pallas_call(
        product_kernel,
        in_specs=[smem] * 5 + [vmem] * 3,
        out_specs=(vmem, vmem),
        out_shape=(
            jax.ShapeDtypeStruct(owned.shape, jnp.float32),
            jax.ShapeDtypeStruct(owned.shape, jnp.bfloat16),
        ),
        cost_estimate=pl.CostEstimate(flops=flops, transcendentals=0, bytes_accessed=nbytes),
        compiler_params=pltpu.CompilerParams(vmem_limit_bytes=48 * 1024 * 1024),
    )(a_t, b_t, v_t, prev_t, misc, rows, cols, owned)


def col_gather(x, grid_cols):
    plus2 = [(j, (j + 2) % grid_cols) for j in range(grid_cols)]
    minus2 = [(j, (j - 2) % grid_cols) for j in range(grid_cols)]
    sib = [(j, j ^ 1) for j in range(grid_cols)]
    half = x.shape[0] // 2
    from_minus = lax.ppermute(x, "col", plus2)
    from_plus = lax.ppermute(x, "col", minus2)
    sib_own = lax.ppermute(x, "col", sib)
    far_a = lax.ppermute(from_minus[:half], "col", plus2)
    far_b = lax.ppermute(from_plus[half:], "col", minus2)
    far = jnp.concatenate([far_a, far_b], axis=0)
    sib_near = lax.ppermute(jnp.stack([from_minus, from_plus]), "col", sib)
    sib_far = lax.ppermute(far, "col", sib)
    pieces = jnp.stack([x, from_minus, from_plus, far, sib_own, sib_near[0], sib_near[1], sib_far])
    return pieces.reshape((-1,) + x.shape[2:])


def piece_classes(col_index, grid_cols):
    j = col_index
    s = j ^ 1
    offs = jnp.stack([j, j - 2, j + 2, j + 4, s, s - 2, s + 2, s + 4])
    return offs % grid_cols


def purify_section(owned, panels, cur_list, next_list, trace_now, grid_rows, grid_cols, row_index, col_index):
    block_rows = owned.shape[0]
    slot_pairs = owned.shape[2]
    edge = owned.shape[4]
    total_rows = cur_list.shape[0]
    slot_count = cur_list.shape[1]
    occupied = total_rows * edge / 2.0
    owned4 = owned.reshape(block_rows, slot_pairs, edge, edge)
    panels = panels.reshape(block_rows, slot_pairs, edge, edge)

    cols = lax.all_gather(panels, "row", axis=0, tiled=False)
    cols = cols.reshape(total_rows * slot_pairs, edge, edge)
    pieces = col_gather(panels, grid_cols)
    zero_slot = pieces.shape[0]
    rows = jnp.concatenate([pieces, jnp.zeros((1, edge, edge), pieces.dtype)])

    cls = piece_classes(col_index, grid_cols)
    piece_of = jnp.zeros((grid_cols,), jnp.int32).at[cls].set(jnp.arange(grid_cols, dtype=jnp.int32))

    my_ids = jnp.arange(block_rows, dtype=jnp.int32) * grid_rows + row_index
    my_cur = cur_list[my_ids]
    my_next = next_list[my_ids]
    out_cols = my_next.reshape(block_rows, slot_pairs, grid_cols)[:, :, col_index]
    k_ids = jnp.arange(slot_count, dtype=jnp.int32)
    k_class = k_ids % grid_cols
    k_pair = k_ids // grid_cols
    a_idx = (piece_of[k_class][None, :] * block_rows + jnp.arange(block_rows, dtype=jnp.int32)[:, None]) * slot_pairs \
        + k_pair[None, :]
    inner = my_cur
    cand = cur_list.reshape(total_rows, slot_pairs, grid_cols)[:, :, col_index][inner]
    match = cand[:, None, :, :] == out_cols[:, :, None, None]
    valid = jnp.any(match, axis=-1)
    lsel = jnp.argmax(match, axis=-1).astype(jnp.int32)
    b_idx = ((inner % grid_rows) * block_rows + inner // grid_rows)[:, None, :] * slot_pairs + lsel
    nout = block_rows * slot_pairs
    a_t = jnp.where(valid, a_idx[:, None, :], zero_slot).reshape(-1)
    b_t = b_idx.reshape(-1)
    v_t = valid.astype(jnp.int32).reshape(-1)

    my_res = my_cur.reshape(block_rows, slot_pairs, grid_cols)[:, :, col_index]
    keep = my_res[:, None, :] == out_cols[:, :, None]
    prev_l = jnp.argmax(keep, axis=-1).astype(jnp.int32)
    prev_t = jnp.where(
        jnp.any(keep, axis=-1), jnp.arange(block_rows, dtype=jnp.int32)[:, None] * slot_pairs + prev_l, -1
    ).reshape(-1)
    misc = (trace_now > occupied).astype(jnp.int32).reshape(1)

    updated, rounded = run_product(a_t, b_t, v_t, prev_t, misc, rows, cols, owned4.reshape(nout, edge, edge))
    return updated.reshape(owned.shape), rounded.reshape(owned.shape)


def local_trace(owned, cur_list, grid_rows, grid_cols, row_index, col_index):
    block_rows = owned.shape[0]
    slot_pairs = owned.shape[2]
    slot_count = cur_list.shape[1]
    own_index = jnp.arange(block_rows, dtype=jnp.int32) * grid_rows + row_index
    my_rows = cur_list[own_index]
    my_residue = my_rows.reshape(block_rows, slot_pairs, grid_cols)[:, :, col_index]
    owned_slots = owned[:, 0, :, 0]
    return jnp.sum(jnp.where(my_residue == own_index[:, None], jnp.trace(owned_slots, axis1=2, axis2=3), 0.0))


def shards(pattern_in, pattern_mid, pattern_out, density_blocks):
    grid_rows = lax.axis_size("row")
    grid_cols = lax.axis_size("col")
    row_index = lax.axis_index("row")
    col_index = lax.axis_index("col")
    all_lists = (pattern_in, pattern_mid, pattern_out)
    current = density_blocks
    rounded = density_blocks.astype(jnp.bfloat16)
    occupied = pattern_in.shape[0] * density_blocks.shape[-1] / 2.0
    diag_term = local_trace(current, pattern_in, grid_rows, grid_cols, row_index, col_index)
    wide = rounded.astype(jnp.float32)
    square_term = jnp.sum(wide * wide)
    totals = lax.psum(lax.psum(jnp.stack([diag_term, square_term]), "col"), "row")
    first_trace = totals[0]
    second_trace = jnp.where(first_trace > occupied, totals[1], 2.0 * first_trace - totals[1])
    traces = (first_trace, second_trace)
    for iteration in range(ITERS):
        current, rounded = purify_section(
            current, rounded, all_lists[iteration], all_lists[iteration + 1], traces[iteration],
            grid_rows, grid_cols, row_index, col_index,
        )
    return current


def solution(mesh):
    in_specs = (P(), P(), P(), P(None, "row", None, "col", None, None))
    out_specs = P(None, "row", None, "col", None, None)
    return jax.shard_map(shards, mesh=mesh, in_specs=in_specs, out_specs=out_specs, check_vma=False)
```

```python
import jax
import jax.numpy as jnp
from jax import lax
from jax.experimental import pallas as pl
from jax.experimental.pallas import tpu as pltpu
from jax.sharding import PartitionSpec as P

ITERS = 2


def product_kernel(a_ref, b_ref, v_ref, prev_ref, misc_ref, rows_hbm, cols_hbm, owned_ref, out_ref, outb_ref,
                   rows_ref, cols_ref, sem):
    nout = out_ref.shape[0]
    terms = a_ref.shape[0] // nout
    take_product = misc_ref[0] > 0
    parts = sem.shape[0] - 1
    step = cols_ref.shape[0] // parts
    copies = [pltpu.make_async_copy(rows_hbm, rows_ref, sem.at[0])]
    for q in range(parts):
        piece = pl.ds(q * step, step)
        copies.append(pltpu.make_async_copy(cols_hbm.at[piece], cols_ref.at[piece], sem.at[q + 1]))
    for c in copies:
        c.start()
    for c in copies:
        c.wait()

    def body(o, carry):
        acc = None
        for k in range(terms):
            t = o * terms + k
            d = jnp.dot(rows_ref[a_ref[t]], cols_ref[b_ref[t]], preferred_element_type=jnp.float32)
            d = jnp.where(v_ref[t] > 0, d, 0.0)
            acc = d if acc is None else acc + d
        p = prev_ref[o]
        prev = jnp.where(p >= 0, owned_ref[jnp.maximum(p, 0)], 0.0)
        res = jnp.where(take_product, acc, 2.0 * prev - acc)
        out_ref[o] = res
        outb_ref[o] = res.astype(outb_ref.dtype)
        return carry

    lax.fori_loop(0, nout, body, 0)


def run_product(a_t, b_t, v_t, prev_t, misc, rows, cols, owned):
    nout, edge, _ = owned.shape
    max_terms = a_t.shape[0]
    smem = pl.BlockSpec(memory_space=pltpu.SMEM)
    vmem = pl.BlockSpec(memory_space=pltpu.VMEM)
    hbm = pl.BlockSpec(memory_space=pl.ANY)
    flops = 2 * edge * edge * edge * max_terms
    nbytes = (rows.size + cols.size) * 2 + 2 * owned.size * 4
    return pl.pallas_call(
        product_kernel,
        in_specs=[smem] * 5 + [hbm, hbm, vmem],
        scratch_shapes=[
            pltpu.VMEM(rows.shape, rows.dtype),
            pltpu.VMEM(cols.shape, cols.dtype),
            pltpu.SemaphoreType.DMA((5,)),
        ],
        out_specs=(vmem, vmem),
        out_shape=(
            jax.ShapeDtypeStruct(owned.shape, jnp.float32),
            jax.ShapeDtypeStruct(owned.shape, jnp.bfloat16),
        ),
        cost_estimate=pl.CostEstimate(flops=flops, transcendentals=0, bytes_accessed=nbytes),
        compiler_params=pltpu.CompilerParams(vmem_limit_bytes=48 * 1024 * 1024),
    )(a_t, b_t, v_t, prev_t, misc, rows, cols, owned)


def col_gather(x, grid_cols):
    plus2 = [(j, (j + 2) % grid_cols) for j in range(grid_cols)]
    minus2 = [(j, (j - 2) % grid_cols) for j in range(grid_cols)]
    sib = [(j, j ^ 1) for j in range(grid_cols)]
    half = x.shape[0] // 2
    from_minus = lax.ppermute(x, "col", plus2)
    from_plus = lax.ppermute(x, "col", minus2)
    sib_own = lax.ppermute(x, "col", sib)
    far_a = lax.ppermute(from_minus[:half], "col", plus2)
    far_b = lax.ppermute(from_plus[half:], "col", minus2)
    far = jnp.concatenate([far_a, far_b], axis=0)
    sib_near = lax.ppermute(jnp.stack([from_minus, from_plus]), "col", sib)
    sib_far = lax.ppermute(far, "col", sib)
    pieces = jnp.stack([x, from_minus, from_plus, far, sib_own, sib_near[0], sib_near[1], sib_far])
    return pieces


def piece_classes(col_index, grid_cols):
    j = col_index
    s = j ^ 1
    offs = jnp.stack([j, j - 2, j + 2, j + 4, s, s - 2, s + 2, s + 4])
    return offs % grid_cols


def purify_section(owned, panels, cur_list, next_list, trace_now, grid_rows, grid_cols, row_index, col_index):
    block_rows = owned.shape[0]
    slot_pairs = owned.shape[2]
    edge = owned.shape[4]
    total_rows = cur_list.shape[0]
    slot_count = cur_list.shape[1]
    occupied = total_rows * edge / 2.0
    owned4 = owned.reshape(block_rows, slot_pairs, edge, edge)
    panels = panels.reshape(block_rows, slot_pairs, edge, edge)

    cols = lax.all_gather(panels, "row", axis=0, tiled=False)
    cols = cols.reshape(total_rows * slot_pairs, edge, edge)
    pieces = col_gather(panels, grid_cols)
    rows = pieces.reshape(grid_cols * block_rows * slot_pairs, edge, edge)

    cls = piece_classes(col_index, grid_cols)
    piece_of = jnp.zeros((grid_cols,), jnp.int32).at[cls].set(jnp.arange(grid_cols, dtype=jnp.int32))

    my_ids = jnp.arange(block_rows, dtype=jnp.int32) * grid_rows + row_index
    my_cur = cur_list[my_ids]
    my_next = next_list[my_ids]
    out_cols = my_next.reshape(block_rows, slot_pairs, grid_cols)[:, :, col_index]
    k_ids = jnp.arange(slot_count, dtype=jnp.int32)
    k_class = k_ids % grid_cols
    k_pair = k_ids // grid_cols
    a_idx = (piece_of[k_class][None, :] * block_rows + jnp.arange(block_rows, dtype=jnp.int32)[:, None]) * slot_pairs \
        + k_pair[None, :]
    inner = my_cur
    cand = cur_list.reshape(total_rows, slot_pairs, grid_cols)[:, :, col_index][inner]
    match = cand[:, None, :, :] == out_cols[:, :, None, None]
    valid = jnp.any(match, axis=-1)
    lsel = jnp.argmax(match, axis=-1).astype(jnp.int32)
    b_idx = ((inner % grid_rows) * block_rows + inner // grid_rows)[:, None, :] * slot_pairs + lsel
    nout = block_rows * slot_pairs
    a_t = jnp.broadcast_to(a_idx[:, None, :], valid.shape).reshape(-1)
    b_t = b_idx.reshape(-1)
    v_t = valid.astype(jnp.int32).reshape(-1)

    my_res = my_cur.reshape(block_rows, slot_pairs, grid_cols)[:, :, col_index]
    keep = my_res[:, None, :] == out_cols[:, :, None]
    prev_l = jnp.argmax(keep, axis=-1).astype(jnp.int32)
    prev_t = jnp.where(
        jnp.any(keep, axis=-1), jnp.arange(block_rows, dtype=jnp.int32)[:, None] * slot_pairs + prev_l, -1
    ).reshape(-1)
    misc = (trace_now > occupied).astype(jnp.int32).reshape(1)

    updated, rounded = run_product(a_t, b_t, v_t, prev_t, misc, rows, cols, owned4.reshape(nout, edge, edge))
    return updated.reshape(owned.shape), rounded.reshape(owned.shape)


def local_trace(owned, cur_list, grid_rows, grid_cols, row_index, col_index):
    block_rows = owned.shape[0]
    slot_pairs = owned.shape[2]
    slot_count = cur_list.shape[1]
    own_index = jnp.arange(block_rows, dtype=jnp.int32) * grid_rows + row_index
    my_rows = cur_list[own_index]
    my_residue = my_rows.reshape(block_rows, slot_pairs, grid_cols)[:, :, col_index]
    owned_slots = owned[:, 0, :, 0]
    return jnp.sum(jnp.where(my_residue == own_index[:, None], jnp.trace(owned_slots, axis1=2, axis2=3), 0.0))


def shards(pattern_in, pattern_mid, pattern_out, density_blocks):
    grid_rows = lax.axis_size("row")
    grid_cols = lax.axis_size("col")
    row_index = lax.axis_index("row")
    col_index = lax.axis_index("col")
    all_lists = (pattern_in, pattern_mid, pattern_out)
    current = density_blocks
    rounded = density_blocks.astype(jnp.bfloat16)
    occupied = pattern_in.shape[0] * density_blocks.shape[-1] / 2.0
    diag_term = local_trace(current, pattern_in, grid_rows, grid_cols, row_index, col_index)
    wide = rounded.astype(jnp.float32)
    square_term = jnp.sum(wide * wide)
    totals = lax.psum(lax.psum(jnp.stack([diag_term, square_term]), "col"), "row")
    first_trace = totals[0]
    second_trace = jnp.where(first_trace > occupied, totals[1], 2.0 * first_trace - totals[1])
    traces = (first_trace, second_trace)
    for iteration in range(ITERS):
        current, rounded = purify_section(
            current, rounded, all_lists[iteration], all_lists[iteration + 1], traces[iteration],
            grid_rows, grid_cols, row_index, col_index,
        )
    return current


def solution(mesh):
    in_specs = (P(), P(), P(), P(None, "row", None, "col", None, None))
    out_specs = P(None, "row", None, "col", None, None)
    return jax.shard_map(shards, mesh=mesh, in_specs=in_specs, out_specs=out_specs, check_vma=False)
```

```python
import jax
import jax.numpy as jnp
from jax import lax
from jax.experimental import pallas as pl
from jax.experimental.pallas import tpu as pltpu
from jax.sharding import PartitionSpec as P

ITERS = 2


def product_kernel(a_ref, b_ref, v_ref, prev_ref, misc_ref, rows_ref, cols_ref, owned_ref, out_ref, *rest):
    nout = out_ref.shape[0]
    terms = a_ref.shape[0] // nout
    take_product = misc_ref[0] > 0

    def body(o, carry):
        sums = [None, None]
        for k in range(terms):
            t = o * terms + k
            d = jnp.dot(rows_ref[a_ref[t]], cols_ref[b_ref[t]], preferred_element_type=jnp.float32)
            d = jnp.where(v_ref[t] > 0, d, 0.0)
            sums[k % 2] = d if sums[k % 2] is None else sums[k % 2] + d
        acc = sums[0] + sums[1]
        p = prev_ref[o]
        prev = jnp.where(p >= 0, owned_ref[jnp.maximum(p, 0)], 0.0)
        res = jnp.where(take_product, acc, 2.0 * prev - acc)
        out_ref[o] = res
        for outb_ref in rest:
            outb_ref[o] = res.astype(outb_ref.dtype)
        return carry

    lax.fori_loop(0, nout, body, 0)


def run_product(a_t, b_t, v_t, prev_t, misc, rows, cols, owned, with_rounded):
    nout, edge, _ = owned.shape
    max_terms = a_t.shape[0]
    smem = pl.BlockSpec(memory_space=pltpu.SMEM)
    vmem = pl.BlockSpec(memory_space=pltpu.VMEM)
    flops = 2 * edge * edge * edge * max_terms
    nbytes = (rows.size + cols.size) * 2 + 2 * owned.size * 4
    return pl.pallas_call(
        product_kernel,
        in_specs=[smem] * 5 + [vmem] * 3,
        out_specs=(vmem,) * (1 + with_rounded),
        out_shape=(jax.ShapeDtypeStruct(owned.shape, jnp.float32),)
        + (jax.ShapeDtypeStruct(owned.shape, jnp.bfloat16),) * with_rounded,
        cost_estimate=pl.CostEstimate(flops=flops, transcendentals=0, bytes_accessed=nbytes),
        compiler_params=pltpu.CompilerParams(vmem_limit_bytes=48 * 1024 * 1024),
    )(a_t, b_t, v_t, prev_t, misc, rows, cols, owned)


def col_gather(x, grid_cols):
    plus2 = [(j, (j + 2) % grid_cols) for j in range(grid_cols)]
    minus2 = [(j, (j - 2) % grid_cols) for j in range(grid_cols)]
    sib = [(j, j ^ 1) for j in range(grid_cols)]
    half = x.shape[0] // 2
    from_minus = lax.ppermute(x, "col", plus2)
    from_plus = lax.ppermute(x, "col", minus2)
    sib_own = lax.ppermute(x, "col", sib)
    far_a = lax.ppermute(from_minus[:half], "col", plus2)
    far_b = lax.ppermute(from_plus[half:], "col", minus2)
    far = jnp.concatenate([far_a, far_b], axis=0)
    sib_near = lax.ppermute(jnp.stack([from_minus, from_plus]), "col", sib)
    sib_far = lax.ppermute(far, "col", sib)
    pieces = jnp.stack([x, from_minus, from_plus, far, sib_own, sib_near[0], sib_near[1], sib_far])
    return pieces


def piece_classes(col_index, grid_cols):
    j = col_index
    s = j ^ 1
    offs = jnp.stack([j, j - 2, j + 2, j + 4, s, s - 2, s + 2, s + 4])
    return offs % grid_cols


def purify_section(owned, panels, cur_list, next_list, trace_now, grid_rows, grid_cols, row_index, col_index, last):
    block_rows = owned.shape[0]
    slot_pairs = owned.shape[2]
    edge = owned.shape[4]
    total_rows = cur_list.shape[0]
    slot_count = cur_list.shape[1]
    occupied = total_rows * edge / 2.0
    owned4 = owned.reshape(block_rows, slot_pairs, edge, edge)
    panels = panels.reshape(block_rows, slot_pairs, edge, edge)

    cols = lax.all_gather(panels, "row", axis=0, tiled=False)
    cols = cols.reshape(total_rows * slot_pairs, edge, edge)
    pieces = col_gather(panels, grid_cols)
    rows = pieces.reshape(grid_cols * block_rows * slot_pairs, edge, edge)

    cls = piece_classes(col_index, grid_cols)
    piece_of = jnp.zeros((grid_cols,), jnp.int32).at[cls].set(jnp.arange(grid_cols, dtype=jnp.int32))

    my_ids = jnp.arange(block_rows, dtype=jnp.int32) * grid_rows + row_index
    my_cur = cur_list[my_ids]
    my_next = next_list[my_ids]
    out_cols = my_next.reshape(block_rows, slot_pairs, grid_cols)[:, :, col_index]
    k_ids = jnp.arange(slot_count, dtype=jnp.int32)
    k_class = k_ids % grid_cols
    k_pair = k_ids // grid_cols
    a_idx = (piece_of[k_class][None, :] * block_rows + jnp.arange(block_rows, dtype=jnp.int32)[:, None]) * slot_pairs \
        + k_pair[None, :]
    inner = my_cur
    cand = cur_list.reshape(total_rows, slot_pairs, grid_cols)[:, :, col_index][inner]
    match = cand[:, None, :, :] == out_cols[:, :, None, None]
    valid = jnp.any(match, axis=-1)
    lsel = jnp.argmax(match, axis=-1).astype(jnp.int32)
    b_idx = ((inner % grid_rows) * block_rows + inner // grid_rows)[:, None, :] * slot_pairs + lsel
    nout = block_rows * slot_pairs
    a_t = jnp.broadcast_to(a_idx[:, None, :], valid.shape).reshape(-1)
    b_t = b_idx.reshape(-1)
    v_t = valid.astype(jnp.int32).reshape(-1)

    my_res = my_cur.reshape(block_rows, slot_pairs, grid_cols)[:, :, col_index]
    keep = my_res[:, None, :] == out_cols[:, :, None]
    prev_l = jnp.argmax(keep, axis=-1).astype(jnp.int32)
    prev_t = jnp.where(
        jnp.any(keep, axis=-1), jnp.arange(block_rows, dtype=jnp.int32)[:, None] * slot_pairs + prev_l, -1
    ).reshape(-1)
    misc = (trace_now > occupied).astype(jnp.int32).reshape(1)

    results = run_product(a_t, b_t, v_t, prev_t, misc, rows, cols, owned4.reshape(nout, edge, edge), int(not last))
    if last:
        return results[0].reshape(owned.shape), None
    return results[0].reshape(owned.shape), results[1].reshape(owned.shape)


def local_trace(owned, cur_list, grid_rows, grid_cols, row_index, col_index):
    block_rows = owned.shape[0]
    slot_pairs = owned.shape[2]
    slot_count = cur_list.shape[1]
    own_index = jnp.arange(block_rows, dtype=jnp.int32) * grid_rows + row_index
    my_rows = cur_list[own_index]
    my_residue = my_rows.reshape(block_rows, slot_pairs, grid_cols)[:, :, col_index]
    owned_slots = owned[:, 0, :, 0]
    return jnp.sum(jnp.where(my_residue == own_index[:, None], jnp.trace(owned_slots, axis1=2, axis2=3), 0.0))


def shards(pattern_in, pattern_mid, pattern_out, density_blocks):
    grid_rows = lax.axis_size("row")
    grid_cols = lax.axis_size("col")
    row_index = lax.axis_index("row")
    col_index = lax.axis_index("col")
    all_lists = (pattern_in, pattern_mid, pattern_out)
    current = density_blocks
    rounded = density_blocks.astype(jnp.bfloat16)
    occupied = pattern_in.shape[0] * density_blocks.shape[-1] / 2.0
    diag_term = local_trace(current, pattern_in, grid_rows, grid_cols, row_index, col_index)
    wide = rounded.astype(jnp.float32)
    square_term = jnp.sum(wide * wide)
    totals = lax.psum(lax.psum(jnp.stack([diag_term, square_term]), "col"), "row")
    first_trace = totals[0]
    second_trace = jnp.where(first_trace > occupied, totals[1], 2.0 * first_trace - totals[1])
    traces = (first_trace, second_trace)
    for iteration in range(ITERS):
        current, rounded = purify_section(
            current, rounded, all_lists[iteration], all_lists[iteration + 1], traces[iteration],
            grid_rows, grid_cols, row_index, col_index, iteration == ITERS - 1,
        )
    return current


def solution(mesh):
    in_specs = (P(), P(), P(), P(None, "row", None, "col", None, None))
    out_specs = P(None, "row", None, "col", None, None)
    return jax.shard_map(shards, mesh=mesh, in_specs=in_specs, out_specs=out_specs, check_vma=False)
```

```python
import jax
import jax.numpy as jnp
from jax import lax
from jax.experimental import pallas as pl
from jax.experimental.pallas import tpu as pltpu
from jax.sharding import PartitionSpec as P

ITERS = 2


def product_kernel(a_ref, b_ref, v_ref, prev_ref, misc_ref, rows_ref, cols_ref, owned_ref, out_ref, outb_ref):
    nout = out_ref.shape[0]
    terms = a_ref.shape[0] // nout
    take_product = misc_ref[0] > 0

    def body(o, carry):
        acc = None
        for k in range(terms):
            t = o * terms + k
            d = jnp.dot(rows_ref[a_ref[t]], cols_ref[b_ref[t]], preferred_element_type=jnp.float32)
            d = jnp.where(v_ref[t] > 0, d, 0.0)
            acc = d if acc is None else acc + d
        p = prev_ref[o]
        prev = jnp.where(p >= 0, owned_ref[jnp.maximum(p, 0)], 0.0)
        res = jnp.where(take_product, acc, 2.0 * prev - acc)
        out_ref[o] = res
        outb_ref[o] = res.astype(outb_ref.dtype)
        return carry

    lax.fori_loop(0, nout, body, 0, unroll=True)


def run_product(a_t, b_t, v_t, prev_t, misc, rows, cols, owned):
    nout, edge, _ = owned.shape
    max_terms = a_t.shape[0]
    smem = pl.BlockSpec(memory_space=pltpu.SMEM)
    vmem = pl.BlockSpec(memory_space=pltpu.VMEM)
    flops = 2 * edge * edge * edge * max_terms
    nbytes = (rows.size + cols.size) * 2 + 2 * owned.size * 4
    return pl.pallas_call(
        product_kernel,
        in_specs=[smem] * 5 + [vmem] * 3,
        out_specs=(vmem, vmem),
        out_shape=(
            jax.ShapeDtypeStruct(owned.shape, jnp.float32),
            jax.ShapeDtypeStruct(owned.shape, jnp.bfloat16),
        ),
        cost_estimate=pl.CostEstimate(flops=flops, transcendentals=0, bytes_accessed=nbytes),
        compiler_params=pltpu.CompilerParams(vmem_limit_bytes=48 * 1024 * 1024),
    )(a_t, b_t, v_t, prev_t, misc, rows, cols, owned)


def col_gather(x, grid_cols):
    plus2 = [(j, (j + 2) % grid_cols) for j in range(grid_cols)]
    minus2 = [(j, (j - 2) % grid_cols) for j in range(grid_cols)]
    sib = [(j, j ^ 1) for j in range(grid_cols)]
    half = x.shape[0] // 2
    from_minus = lax.ppermute(x, "col", plus2)
    from_plus = lax.ppermute(x, "col", minus2)
    sib_own = lax.ppermute(x, "col", sib)
    far_a = lax.ppermute(from_minus[:half], "col", plus2)
    far_b = lax.ppermute(from_plus[half:], "col", minus2)
    far = jnp.concatenate([far_a, far_b], axis=0)
    sib_near = lax.ppermute(jnp.stack([from_minus, from_plus]), "col", sib)
    sib_far = lax.ppermute(far, "col", sib)
    pieces = jnp.stack([x, from_minus, from_plus, far, sib_own, sib_near[0], sib_near[1], sib_far])
    return pieces


def piece_classes(col_index, grid_cols):
    j = col_index
    s = j ^ 1
    offs = jnp.stack([j, j - 2, j + 2, j + 4, s, s - 2, s + 2, s + 4])
    return offs % grid_cols


def purify_section(owned, panels, cur_list, next_list, trace_now, grid_rows, grid_cols, row_index, col_index):
    block_rows = owned.shape[0]
    slot_pairs = owned.shape[2]
    edge = owned.shape[4]
    total_rows = cur_list.shape[0]
    slot_count = cur_list.shape[1]
    occupied = total_rows * edge / 2.0
    owned4 = owned.reshape(block_rows, slot_pairs, edge, edge)
    panels = panels.reshape(block_rows, slot_pairs, edge, edge)

    cols = lax.all_gather(panels, "row", axis=0, tiled=False)
    cols = cols.reshape(total_rows * slot_pairs, edge, edge)
    pieces = col_gather(panels, grid_cols)
    rows = pieces.reshape(grid_cols * block_rows * slot_pairs, edge, edge)

    cls = piece_classes(col_index, grid_cols)
    piece_of = jnp.zeros((grid_cols,), jnp.int32).at[cls].set(jnp.arange(grid_cols, dtype=jnp.int32))

    my_ids = jnp.arange(block_rows, dtype=jnp.int32) * grid_rows + row_index
    my_cur = cur_list[my_ids]
    my_next = next_list[my_ids]
    out_cols = my_next.reshape(block_rows, slot_pairs, grid_cols)[:, :, col_index]
    k_ids = jnp.arange(slot_count, dtype=jnp.int32)
    k_class = k_ids % grid_cols
    k_pair = k_ids // grid_cols
    a_idx = (piece_of[k_class][None, :] * block_rows + jnp.arange(block_rows, dtype=jnp.int32)[:, None]) * slot_pairs \
        + k_pair[None, :]
    inner = my_cur
    cand = cur_list.reshape(total_rows, slot_pairs, grid_cols)[:, :, col_index][inner]
    match = cand[:, None, :, :] == out_cols[:, :, None, None]
    valid = jnp.any(match, axis=-1)
    lsel = jnp.argmax(match, axis=-1).astype(jnp.int32)
    b_idx = ((inner % grid_rows) * block_rows + inner // grid_rows)[:, None, :] * slot_pairs + lsel
    nout = block_rows * slot_pairs
    a_t = jnp.broadcast_to(a_idx[:, None, :], valid.shape).reshape(-1)
    b_t = b_idx.reshape(-1)
    v_t = valid.astype(jnp.int32).reshape(-1)

    my_res = my_cur.reshape(block_rows, slot_pairs, grid_cols)[:, :, col_index]
    keep = my_res[:, None, :] == out_cols[:, :, None]
    prev_l = jnp.argmax(keep, axis=-1).astype(jnp.int32)
    prev_t = jnp.where(
        jnp.any(keep, axis=-1), jnp.arange(block_rows, dtype=jnp.int32)[:, None] * slot_pairs + prev_l, -1
    ).reshape(-1)
    misc = (trace_now > occupied).astype(jnp.int32).reshape(1)

    updated, rounded = run_product(a_t, b_t, v_t, prev_t, misc, rows, cols, owned4.reshape(nout, edge, edge))
    return updated.reshape(owned.shape), rounded.reshape(owned.shape)


def local_trace(owned, cur_list, grid_rows, grid_cols, row_index, col_index):
    block_rows = owned.shape[0]
    slot_pairs = owned.shape[2]
    slot_count = cur_list.shape[1]
    own_index = jnp.arange(block_rows, dtype=jnp.int32) * grid_rows + row_index
    my_rows = cur_list[own_index]
    my_residue = my_rows.reshape(block_rows, slot_pairs, grid_cols)[:, :, col_index]
    owned_slots = owned[:, 0, :, 0]
    return jnp.sum(jnp.where(my_residue == own_index[:, None], jnp.trace(owned_slots, axis1=2, axis2=3), 0.0))


def shards(pattern_in, pattern_mid, pattern_out, density_blocks):
    grid_rows = lax.axis_size("row")
    grid_cols = lax.axis_size("col")
    row_index = lax.axis_index("row")
    col_index = lax.axis_index("col")
    all_lists = (pattern_in, pattern_mid, pattern_out)
    current = density_blocks
    rounded = density_blocks.astype(jnp.bfloat16)
    occupied = pattern_in.shape[0] * density_blocks.shape[-1] / 2.0
    diag_term = local_trace(current, pattern_in, grid_rows, grid_cols, row_index, col_index)
    wide = rounded.astype(jnp.float32)
    square_term = jnp.sum(wide * wide)
    totals = lax.psum(lax.psum(jnp.stack([diag_term, square_term]), "col"), "row")
    first_trace = totals[0]
    second_trace = jnp.where(first_trace > occupied, totals[1], 2.0 * first_trace - totals[1])
    traces = (first_trace, second_trace)
    for iteration in range(ITERS):
        current, rounded = purify_section(
            current, rounded, all_lists[iteration], all_lists[iteration + 1], traces[iteration],
            grid_rows, grid_cols, row_index, col_index,
        )
    return current


def solution(mesh):
    in_specs = (P(), P(), P(), P(None, "row", None, "col", None, None))
    out_specs = P(None, "row", None, "col", None, None)
    return jax.shard_map(shards, mesh=mesh, in_specs=in_specs, out_specs=out_specs, check_vma=False)
```

```python
import jax
import jax.numpy as jnp
from jax import lax
from jax.experimental import pallas as pl
from jax.experimental.pallas import tpu as pltpu
from jax.sharding import PartitionSpec as P

ITERS = 2


def product_kernel(a_ref, b_ref, v_ref, prev_ref, misc_ref, rows_ref, cols_ref, owned_ref, out_ref, *rest):
    nout = out_ref.shape[0]
    terms = a_ref.shape[0] // nout
    take_product = misc_ref[0] > 0

    def body(o, carry):
        acc = None
        for k in range(terms):
            t = o * terms + k
            d = jnp.dot(rows_ref[a_ref[t]], cols_ref[b_ref[t]], preferred_element_type=jnp.float32)
            d = jnp.where(v_ref[t] > 0, d, 0.0)
            acc = d if acc is None else acc + d
        p = prev_ref[o]
        prev = jnp.where(p >= 0, owned_ref[jnp.maximum(p, 0)], 0.0)
        res = jnp.where(take_product, acc, 2.0 * prev - acc)
        out_ref[o] = res
        for outb_ref in rest:
            outb_ref[o] = res.astype(outb_ref.dtype)
        return carry

    lax.fori_loop(0, nout, body, 0, unroll=True)


def run_product(a_t, b_t, v_t, prev_t, misc, rows, cols, owned, with_rounded):
    nout, edge, _ = owned.shape
    max_terms = a_t.shape[0]
    smem = pl.BlockSpec(memory_space=pltpu.SMEM)
    vmem = pl.BlockSpec(memory_space=pltpu.VMEM)
    flops = 2 * edge * edge * edge * max_terms
    nbytes = (rows.size + cols.size) * 2 + 2 * owned.size * 4
    return pl.pallas_call(
        product_kernel,
        in_specs=[smem] * 5 + [vmem] * 3,
        out_specs=(vmem,) * (1 + with_rounded),
        out_shape=(jax.ShapeDtypeStruct(owned.shape, jnp.float32),)
        + (jax.ShapeDtypeStruct(owned.shape, jnp.bfloat16),) * with_rounded,
        cost_estimate=pl.CostEstimate(flops=flops, transcendentals=0, bytes_accessed=nbytes),
        compiler_params=pltpu.CompilerParams(vmem_limit_bytes=48 * 1024 * 1024),
    )(a_t, b_t, v_t, prev_t, misc, rows, cols, owned)


def col_gather(x, grid_cols):
    plus2 = [(j, (j + 2) % grid_cols) for j in range(grid_cols)]
    minus2 = [(j, (j - 2) % grid_cols) for j in range(grid_cols)]
    sib = [(j, j ^ 1) for j in range(grid_cols)]
    half = x.shape[0] // 2
    from_minus = lax.ppermute(x, "col", plus2)
    from_plus = lax.ppermute(x, "col", minus2)
    sib_own = lax.ppermute(x, "col", sib)
    far_a = lax.ppermute(from_minus[:half], "col", plus2)
    far_b = lax.ppermute(from_plus[half:], "col", minus2)
    far = jnp.concatenate([far_a, far_b], axis=0)
    sib_near = lax.ppermute(jnp.stack([from_minus, from_plus]), "col", sib)
    sib_far = lax.ppermute(far, "col", sib)
    pieces = jnp.stack([x, from_minus, from_plus, far, sib_own, sib_near[0], sib_near[1], sib_far])
    return pieces


def piece_classes(col_index, grid_cols):
    j = col_index
    s = j ^ 1
    offs = jnp.stack([j, j - 2, j + 2, j + 4, s, s - 2, s + 2, s + 4])
    return offs % grid_cols


def purify_section(owned, panels, cur_list, next_list, trace_now, grid_rows, grid_cols, row_index, col_index, last):
    block_rows = owned.shape[0]
    slot_pairs = owned.shape[2]
    edge = owned.shape[4]
    total_rows = cur_list.shape[0]
    slot_count = cur_list.shape[1]
    occupied = total_rows * edge / 2.0
    owned4 = owned.reshape(block_rows, slot_pairs, edge, edge)
    panels = panels.reshape(block_rows, slot_pairs, edge, edge)

    cols = lax.all_gather(panels, "row", axis=0, tiled=False)
    cols = cols.reshape(total_rows * slot_pairs, edge, edge)
    pieces = col_gather(panels, grid_cols)
    rows = pieces.reshape(grid_cols * block_rows * slot_pairs, edge, edge)

    cls = piece_classes(col_index, grid_cols)
    piece_of = jnp.zeros((grid_cols,), jnp.int32).at[cls].set(jnp.arange(grid_cols, dtype=jnp.int32))

    my_ids = jnp.arange(block_rows, dtype=jnp.int32) * grid_rows + row_index
    my_cur = cur_list[my_ids]
    my_next = next_list[my_ids]
    out_cols = my_next.reshape(block_rows, slot_pairs, grid_cols)[:, :, col_index]
    k_ids = jnp.arange(slot_count, dtype=jnp.int32)
    k_class = k_ids % grid_cols
    k_pair = k_ids // grid_cols
    a_idx = (piece_of[k_class][None, :] * block_rows + jnp.arange(block_rows, dtype=jnp.int32)[:, None]) * slot_pairs \
        + k_pair[None, :]
    inner = my_cur
    cand = cur_list.reshape(total_rows, slot_pairs, grid_cols)[:, :, col_index][inner]
    match = cand[:, None, :, :] == out_cols[:, :, None, None]
    valid = jnp.any(match, axis=-1)
    lsel = jnp.argmax(match, axis=-1).astype(jnp.int32)
    b_idx = ((inner % grid_rows) * block_rows + inner // grid_rows)[:, None, :] * slot_pairs + lsel
    nout = block_rows * slot_pairs
    a_t = jnp.broadcast_to(a_idx[:, None, :], valid.shape).reshape(-1)
    b_t = b_idx.reshape(-1)
    v_t = valid.astype(jnp.int32).reshape(-1)

    my_res = my_cur.reshape(block_rows, slot_pairs, grid_cols)[:, :, col_index]
    keep = my_res[:, None, :] == out_cols[:, :, None]
    prev_l = jnp.argmax(keep, axis=-1).astype(jnp.int32)
    prev_t = jnp.where(
        jnp.any(keep, axis=-1), jnp.arange(block_rows, dtype=jnp.int32)[:, None] * slot_pairs + prev_l, -1
    ).reshape(-1)
    misc = (trace_now > occupied).astype(jnp.int32).reshape(1)

    results = run_product(a_t, b_t, v_t, prev_t, misc, rows, cols, owned4.reshape(nout, edge, edge), int(not last))
    if last:
        return results[0].reshape(owned.shape), None
    return results[0].reshape(owned.shape), results[1].reshape(owned.shape)


def local_trace(owned, cur_list, grid_rows, grid_cols, row_index, col_index):
    block_rows = owned.shape[0]
    slot_pairs = owned.shape[2]
    slot_count = cur_list.shape[1]
    own_index = jnp.arange(block_rows, dtype=jnp.int32) * grid_rows + row_index
    my_rows = cur_list[own_index]
    my_residue = my_rows.reshape(block_rows, slot_pairs, grid_cols)[:, :, col_index]
    owned_slots = owned[:, 0, :, 0]
    return jnp.sum(jnp.where(my_residue == own_index[:, None], jnp.trace(owned_slots, axis1=2, axis2=3), 0.0))


def shards(pattern_in, pattern_mid, pattern_out, density_blocks):
    grid_rows = lax.axis_size("row")
    grid_cols = lax.axis_size("col")
    row_index = lax.axis_index("row")
    col_index = lax.axis_index("col")
    all_lists = (pattern_in, pattern_mid, pattern_out)
    current = density_blocks
    rounded = density_blocks.astype(jnp.bfloat16)
    occupied = pattern_in.shape[0] * density_blocks.shape[-1] / 2.0
    diag_term = local_trace(current, pattern_in, grid_rows, grid_cols, row_index, col_index)
    wide = rounded.astype(jnp.float32)
    square_term = jnp.sum(wide * wide)
    totals = lax.psum(lax.psum(jnp.stack([diag_term, square_term]), "col"), "row")
    first_trace = totals[0]
    second_trace = jnp.where(first_trace > occupied, totals[1], 2.0 * first_trace - totals[1])
    traces = (first_trace, second_trace)
    for iteration in range(ITERS):
        current, rounded = purify_section(
            current, rounded, all_lists[iteration], all_lists[iteration + 1], traces[iteration],
            grid_rows, grid_cols, row_index, col_index, iteration == ITERS - 1,
        )
    return current


def solution(mesh):
    in_specs = (P(), P(), P(), P(None, "row", None, "col", None, None))
    out_specs = P(None, "row", None, "col", None, None)
    return jax.shard_map(shards, mesh=mesh, in_specs=in_specs, out_specs=out_specs, check_vma=False)
```

```python
import jax
import jax.numpy as jnp
from jax import lax
from jax.experimental import pallas as pl
from jax.experimental.pallas import tpu as pltpu
from jax.sharding import PartitionSpec as P

ITERS = 2


def product_kernel(a_ref, b_ref, v_ref, prev_ref, misc_ref, rows_ref, cols_ref, owned_ref, out_ref, *rest):
    nout = out_ref.shape[0]
    terms = a_ref.shape[0] // nout
    take_product = misc_ref[0] > 0

    def body(o, carry):
        acc = None
        for k in range(terms):
            t = o * terms + k
            lhs = jnp.where(v_ref[t] > 0, rows_ref[a_ref[t]], jnp.zeros((), rows_ref.dtype))
            d = jnp.dot(lhs, cols_ref[b_ref[t]], preferred_element_type=jnp.float32)
            acc = d if acc is None else acc + d
        p = prev_ref[o]
        prev = jnp.where(p >= 0, owned_ref[jnp.maximum(p, 0)], 0.0)
        res = jnp.where(take_product, acc, 2.0 * prev - acc)
        out_ref[o] = res
        for outb_ref in rest:
            outb_ref[o] = res.astype(outb_ref.dtype)
        return carry

    lax.fori_loop(0, nout, body, 0, unroll=True)


def run_product(a_t, b_t, v_t, prev_t, misc, rows, cols, owned, with_rounded):
    nout, edge, _ = owned.shape
    max_terms = a_t.shape[0]
    smem = pl.BlockSpec(memory_space=pltpu.SMEM)
    vmem = pl.BlockSpec(memory_space=pltpu.VMEM)
    flops = 2 * edge * edge * edge * max_terms
    nbytes = (rows.size + cols.size) * 2 + 2 * owned.size * 4
    return pl.pallas_call(
        product_kernel,
        in_specs=[smem] * 5 + [vmem] * 3,
        out_specs=(vmem,) * (1 + with_rounded),
        out_shape=(jax.ShapeDtypeStruct(owned.shape, jnp.float32),)
        + (jax.ShapeDtypeStruct(owned.shape, jnp.bfloat16),) * with_rounded,
        cost_estimate=pl.CostEstimate(flops=flops, transcendentals=0, bytes_accessed=nbytes),
        compiler_params=pltpu.CompilerParams(vmem_limit_bytes=48 * 1024 * 1024),
    )(a_t, b_t, v_t, prev_t, misc, rows, cols, owned)


def col_gather(x, grid_cols):
    plus2 = [(j, (j + 2) % grid_cols) for j in range(grid_cols)]
    minus2 = [(j, (j - 2) % grid_cols) for j in range(grid_cols)]
    sib = [(j, j ^ 1) for j in range(grid_cols)]
    half = x.shape[0] // 2
    from_minus = lax.ppermute(x, "col", plus2)
    from_plus = lax.ppermute(x, "col", minus2)
    sib_own = lax.ppermute(x, "col", sib)
    far_a = lax.ppermute(from_minus[:half], "col", plus2)
    far_b = lax.ppermute(from_plus[half:], "col", minus2)
    far = jnp.concatenate([far_a, far_b], axis=0)
    sib_near = lax.ppermute(jnp.stack([from_minus, from_plus]), "col", sib)
    sib_far = lax.ppermute(far, "col", sib)
    pieces = jnp.stack([x, from_minus, from_plus, far, sib_own, sib_near[0], sib_near[1], sib_far])
    return pieces


def piece_classes(col_index, grid_cols):
    j = col_index
    s = j ^ 1
    offs = jnp.stack([j, j - 2, j + 2, j + 4, s, s - 2, s + 2, s + 4])
    return offs % grid_cols


def purify_section(owned, panels, cur_list, next_list, trace_now, grid_rows, grid_cols, row_index, col_index, last):
    block_rows = owned.shape[0]
    slot_pairs = owned.shape[2]
    edge = owned.shape[4]
    total_rows = cur_list.shape[0]
    slot_count = cur_list.shape[1]
    occupied = total_rows * edge / 2.0
    owned4 = owned.reshape(block_rows, slot_pairs, edge, edge)
    panels = panels.reshape(block_rows, slot_pairs, edge, edge)

    cols = lax.all_gather(panels, "row", axis=0, tiled=False)
    cols = cols.reshape(total_rows * slot_pairs, edge, edge)
    pieces = col_gather(panels, grid_cols)
    rows = pieces.reshape(grid_cols * block_rows * slot_pairs, edge, edge)

    cls = piece_classes(col_index, grid_cols)
    piece_of = jnp.zeros((grid_cols,), jnp.int32).at[cls].set(jnp.arange(grid_cols, dtype=jnp.int32))

    my_ids = jnp.arange(block_rows, dtype=jnp.int32) * grid_rows + row_index
    my_cur = cur_list[my_ids]
    my_next = next_list[my_ids]
    out_cols = my_next.reshape(block_rows, slot_pairs, grid_cols)[:, :, col_index]
    k_ids = jnp.arange(slot_count, dtype=jnp.int32)
    k_class = k_ids % grid_cols
    k_pair = k_ids // grid_cols
    a_idx = (piece_of[k_class][None, :] * block_rows + jnp.arange(block_rows, dtype=jnp.int32)[:, None]) * slot_pairs \
        + k_pair[None, :]
    inner = my_cur
    cand = cur_list.reshape(total_rows, slot_pairs, grid_cols)[:, :, col_index][inner]
    match = cand[:, None, :, :] == out_cols[:, :, None, None]
    valid = jnp.any(match, axis=-1)
    lsel = jnp.argmax(match, axis=-1).astype(jnp.int32)
    b_idx = ((inner % grid_rows) * block_rows + inner // grid_rows)[:, None, :] * slot_pairs + lsel
    nout = block_rows * slot_pairs
    a_t = jnp.broadcast_to(a_idx[:, None, :], valid.shape).reshape(-1)
    b_t = b_idx.reshape(-1)
    v_t = valid.astype(jnp.int32).reshape(-1)

    my_res = my_cur.reshape(block_rows, slot_pairs, grid_cols)[:, :, col_index]
    keep = my_res[:, None, :] == out_cols[:, :, None]
    prev_l = jnp.argmax(keep, axis=-1).astype(jnp.int32)
    prev_t = jnp.where(
        jnp.any(keep, axis=-1), jnp.arange(block_rows, dtype=jnp.int32)[:, None] * slot_pairs + prev_l, -1
    ).reshape(-1)
    misc = (trace_now > occupied).astype(jnp.int32).reshape(1)

    results = run_product(a_t, b_t, v_t, prev_t, misc, rows, cols, owned4.reshape(nout, edge, edge), int(not last))
    if last:
        return results[0].reshape(owned.shape), None
    return results[0].reshape(owned.shape), results[1].reshape(owned.shape)


def local_trace(owned, cur_list, grid_rows, grid_cols, row_index, col_index):
    block_rows = owned.shape[0]
    slot_pairs = owned.shape[2]
    slot_count = cur_list.shape[1]
    own_index = jnp.arange(block_rows, dtype=jnp.int32) * grid_rows + row_index
    my_rows = cur_list[own_index]
    my_residue = my_rows.reshape(block_rows, slot_pairs, grid_cols)[:, :, col_index]
    owned_slots = owned[:, 0, :, 0]
    return jnp.sum(jnp.where(my_residue == own_index[:, None], jnp.trace(owned_slots, axis1=2, axis2=3), 0.0))


def shards(pattern_in, pattern_mid, pattern_out, density_blocks):
    grid_rows = lax.axis_size("row")
    grid_cols = lax.axis_size("col")
    row_index = lax.axis_index("row")
    col_index = lax.axis_index("col")
    all_lists = (pattern_in, pattern_mid, pattern_out)
    current = density_blocks
    rounded = density_blocks.astype(jnp.bfloat16)
    occupied = pattern_in.shape[0] * density_blocks.shape[-1] / 2.0
    diag_term = local_trace(current, pattern_in, grid_rows, grid_cols, row_index, col_index)
    wide = rounded.astype(jnp.float32)
    square_term = jnp.sum(wide * wide)
    totals = lax.psum(lax.psum(jnp.stack([diag_term, square_term]), "col"), "row")
    first_trace = totals[0]
    second_trace = jnp.where(first_trace > occupied, totals[1], 2.0 * first_trace - totals[1])
    traces = (first_trace, second_trace)
    for iteration in range(ITERS):
        current, rounded = purify_section(
            current, rounded, all_lists[iteration], all_lists[iteration + 1], traces[iteration],
            grid_rows, grid_cols, row_index, col_index, iteration == ITERS - 1,
        )
    return current


def solution(mesh):
    in_specs = (P(), P(), P(), P(None, "row", None, "col", None, None))
    out_specs = P(None, "row", None, "col", None, None)
    return jax.shard_map(shards, mesh=mesh, in_specs=in_specs, out_specs=out_specs, check_vma=False)
```
